256 devices in a mesh: ctx: 16 (over x, y), tp: 16 (over z, core).
Axes of the slice: x: 4, y: 4, z: 8, core: 2. Of those that a mesh axis runs over, the one named last changes fastest.
Arguments:
- tokens: bfloat16 [16384, 2560], P(('ctx', 'tp')), may hold values from -8 to 8
- norm1_gain: float32 [2560], replicated, may hold values from 0.1 to 1.9
- w_z: bfloat16 [2560, 5120], P(None, 'tp'), may hold values from -0.125 to 0.125
- w_x: bfloat16 [2560, 5120], P(None, 'tp'), may hold values from -0.125 to 0.125
- w_bc: bfloat16 [2560, 256], replicated, may hold values from -0.125 to 0.125
- w_dt: bfloat16 [2560, 80], P(None, 'tp'), may hold values from -1 to 1
- dt_bias: float32 [80], P('tp'), may hold values from -5.5 to -4
- a_log: float32 [80], P('tp'), may hold values from -12 to 1.4
- conv_x: float32 [4, 5120], P(None, 'tp'), may hold values from -3 to 3
- conv_bc: float32 [4, 256], replicated, may hold values from -3 to 3
- d_skip: float32 [80], P('tp'), may hold values from 0.1 to 1.9
- ssm_gain: float32 [5120], P('tp'), may hold values from 0.1 to 1.9
- w_out: bfloat16 [5120, 2560], P('tp'), may hold values from -0.078125 to 0.078125
- norm2_gain: float32 [2560], replicated, may hold values from 0.1 to 1.9
- w_gate: bfloat16 [2560, 5120], P(None, 'tp'), may hold values from -0.125 to 0.125
- w_up: bfloat16 [2560, 5120], P(None, 'tp'), may hold values from -0.125 to 0.125
- w_down: bfloat16 [5120, 2560], P('tp'), may hold values from -0.078125 to 0.078125
Outputs:
- layer_out: bfloat16 [16384, 2560], P(('ctx', 'tp'))
The draws below stay inside these ranges and needn't reach their ends.
All inputs are finite; a program needn't handle non-finite values.
Results may differ from the reference program's by a relative error of at most 0.017.
Values may be sent and summed in bfloat16 or wider, within the bound.
No kernel may reach another device: no remote copies, remote signals or barrier semaphores. Data moves between devices by JAX's collectives and lax.ppermute only.
A program may use at most 128 MiB of HBM per device.

```python
import math
import jax
import jax.numpy as jnp
from jax import lax

WIDTH = 2560
HEADS = 80
HEAD_DIM = 64
STATE_DIM = 128
MLP_DIM = 5120
BLOCK_LEN = 256
TOK_DEV = 1024
SEQ_LEN = 16384
N_TP = 16


def draw_a_log(key, part):
    key_pick, key_fast, key_slow = jax.random.split(key, 3)
    share = 0.5
    picker = jax.random.uniform(key_pick, (HEADS,), dtype=jnp.float32)
    fast_rate = jnp.exp(jax.random.uniform(key_fast, (HEADS,), dtype=jnp.float32, minval=math.log(1.5), maxval=math.log(4.0)))
    slow_rate = jax.random.uniform(key_slow, (HEADS,), dtype=jnp.float32, minval=0.05, maxval=1.0) * (100.0 / SEQ_LEN)
    chosen = jnp.where(picker < share, fast_rate, slow_rate)
    return jnp.log(chosen).astype(jnp.float32)


def common_direction(key):
    raw = jax.random.normal(jax.random.fold_in(key, 7), (WIDTH,), dtype=jnp.float32)
    return raw * lax_rsqrt_sum(raw)


def lax_rsqrt_sum(raw):
    return 1.0 / jnp.sqrt(jnp.sum(raw * raw))


def draw_w_dt(key, part):
    direction = common_direction(key)
    noise = jax.random.normal(jax.random.fold_in(key, 11), (WIDTH, HEADS), dtype=jnp.float32) / math.sqrt(WIDTH)
    loads = jax.random.uniform(jax.random.fold_in(key, 19), (HEADS,), dtype=jnp.float32, minval=-3.0, maxval=3.0) / math.sqrt(WIDTH)
    result = noise + direction[:, None] * loads[None, :]
    return jnp.clip(result, -1.0, 1.0).astype(jnp.bfloat16)


def draw_tokens(key, part):
    direction = common_direction(key)
    noise = jax.random.normal(jax.random.fold_in(key, 13), (SEQ_LEN, WIDTH), dtype=jnp.float32)
    group_shift = jax.random.uniform(jax.random.fold_in(key, 17), (SEQ_LEN // TOK_DEV,), dtype=jnp.float32, minval=-3.0, maxval=3.0)
    per_row = jnp.repeat(group_shift, TOK_DEV)
    result = noise + per_row[:, None] * (math.sqrt(WIDTH) * direction)[None, :]
    return jnp.clip(result, -8.0, 8.0).astype(jnp.bfloat16)


def levels(stream_key, extent, cuts, least, high):
    def one(axis_at, parts):
        heights = jax.random.uniform(jax.random.fold_in(jax.random.fold_in(stream_key, 6), axis_at), (parts,), jnp.float32, least / len(cuts), high / len(cuts))
        return jnp.repeat(jnp.exp(heights), extent[axis_at] // parts).reshape((-1,) + (1,) * (len(extent) - axis_at - 1))

    level = one(*cuts[0])
    for cut in cuts[1:]:
        level = level * one(*cut)
    return level


def scatter_about(stream_key, extent, width, most, shards=(), kind=jnp.bfloat16):
    drawn = width * jax.random.normal(stream_key, extent, jnp.float32)
    if shards:
        drawn = drawn * levels(stream_key, extent, shards, -0.22, 0.18)
    return jnp.clip(drawn, -most, most).astype(kind)


def setup_inputs(seed: int = 0) -> dict:
    key_list = jax.random.split(jax.random.key(seed), 18)
    tokens = draw_tokens(jax.random.fold_in(key_list[17], 71), 0)
    norm1_gain = jnp.clip(1.0 + 0.18 * jax.random.normal(key_list[1], (WIDTH,), jnp.float32), 0.1, 1.9)
    w_z = scatter_about(key_list[2], (WIDTH, HEADS * HEAD_DIM), WIDTH ** -0.5, 0.125, ((1, 16),))
    w_x = scatter_about(key_list[3], (WIDTH, HEADS * HEAD_DIM), WIDTH ** -0.5, 0.125, ((1, 16),))
    w_bc = scatter_about(key_list[4], (WIDTH, 2 * STATE_DIM), WIDTH ** -0.5, 0.125)
    w_dt = draw_w_dt(jax.random.fold_in(key_list[17], 71), 0)
    dt_bias = jnp.clip(-5.5 + 1.5 * jax.random.uniform(key_list[6], (HEADS,), jnp.float32) ** levels(key_list[6], (HEADS,), ((0, 16),), -0.2, 0.2), -5.5, -4.0)
    a_log = draw_a_log(jax.random.fold_in(key_list[17], 71), 0)
    conv_x = scatter_about(key_list[8], (4, HEADS * HEAD_DIM), 4 ** -0.5, 3.0, ((1, 16),), jnp.float32)
    conv_bc = scatter_about(key_list[9], (4, 2 * STATE_DIM), 4 ** -0.5, 3.0, (), jnp.float32)
    d_skip = jnp.clip(1.0 + 0.18 * jax.random.normal(key_list[10], (HEADS,), jnp.float32), 0.1, 1.9)
    ssm_gain = jnp.clip(1.0 + 0.18 * jax.random.normal(key_list[11], (HEADS * HEAD_DIM,), jnp.float32), 0.1, 1.9)
    w_out = scatter_about(key_list[12], (HEADS * HEAD_DIM, WIDTH), (HEADS * HEAD_DIM) ** -0.5, 0.078125, ((0, 16),))
    norm2_gain = jnp.clip(1.0 + 0.18 * jax.random.normal(key_list[13], (WIDTH,), jnp.float32), 0.1, 1.9)
    w_gate = scatter_about(key_list[14], (WIDTH, MLP_DIM), WIDTH ** -0.5, 0.125, ((1, 16),))
    w_up = scatter_about(key_list[15], (WIDTH, MLP_DIM), WIDTH ** -0.5, 0.125, ((1, 16),))
    w_down = scatter_about(key_list[16], (MLP_DIM, WIDTH), MLP_DIM ** -0.5, 0.078125, ((0, 16),))
    return dict(tokens=tokens, norm1_gain=norm1_gain, w_z=w_z, w_x=w_x, w_bc=w_bc, w_dt=w_dt, dt_bias=dt_bias, a_log=a_log, conv_x=conv_x, conv_bc=conv_bc, d_skip=d_skip, ssm_gain=ssm_gain, w_out=w_out, norm2_gain=norm2_gain, w_gate=w_gate, w_up=w_up, w_down=w_down)


EPS = 1e-05

def rms_rows(values, gain):
    wide = values.astype(jnp.float32)
    return wide * lax.rsqrt(lax.optimization_barrier(jnp.mean(wide * wide, axis=-1, keepdims=True)) + EPS) * gain

def conv_four(rim, current, kernel):
    extended = jnp.concatenate([rim, current], axis=0).astype(jnp.float32)
    length = current.shape[0]
    result = kernel[0] * extended[0:length]
    for offset in range(1, 4):
        result = result + kernel[offset] * extended[offset:offset + length]
    return result

def split_sum(left, right):
    groups = N_TP
    inner_len = left.shape[1] // groups
    left_parts = left.reshape(left.shape[0], groups, inner_len).astype(jnp.float32)
    right_parts = right.reshape(groups, inner_len, right.shape[1]).astype(jnp.float32)
    partial_sums = jnp.einsum('tkc,kcd->ktd', left_parts, right_parts).astype(jnp.bfloat16)
    partial_sums = lax.optimization_barrier(partial_sums)
    return lax.optimization_barrier(jnp.sum(partial_sums.astype(jnp.float32), axis=0))

def reference(tokens, norm1_gain, w_z, w_x, w_bc, w_dt, dt_bias, a_log, conv_x, conv_bc, d_skip, ssm_gain, w_out, norm2_gain, w_gate, w_up, w_down):
    block_count = SEQ_LEN // BLOCK_LEN
    channels = HEADS * HEAD_DIM
    causal_mask = jnp.tril(jnp.ones((BLOCK_LEN, BLOCK_LEN), dtype=bool))

    def block_step(carry, block_tokens):
        state, rim_inner, rim_bc = carry
        normed = rms_rows(block_tokens, norm1_gain).astype(jnp.bfloat16)
        gate_z = jnp.dot(normed, w_z, preferred_element_type=jnp.float32)
        inner_rows = jnp.dot(normed, w_x, preferred_element_type=jnp.float32).astype(jnp.bfloat16)
        bc_rows = jnp.dot(normed, w_bc, preferred_element_type=jnp.float32).astype(jnp.bfloat16)
        dt_raw = jnp.dot(normed, w_dt, preferred_element_type=jnp.float32)
        conv_inner = jax.nn.silu(conv_four(rim_inner, inner_rows, conv_x)).astype(jnp.bfloat16)
        conv_bcm = jax.nn.silu(conv_four(rim_bc, bc_rows, conv_bc)).astype(jnp.bfloat16)
        dt_step = jax.nn.softplus(dt_raw + dt_bias)
        log_decay = -dt_step * jnp.exp(a_log)
        cum_decay = jnp.cumsum(log_decay, axis=0)
        b_mat = conv_bcm[:, :STATE_DIM]
        c_mat = conv_bcm[:, STATE_DIM:]
        scores = jnp.dot(c_mat, b_mat.T, preferred_element_type=jnp.float32)
        decay_diff = jnp.where(causal_mask[:, :, None], cum_decay[:, None, :] - cum_decay[None, :, :], 0.0)
        weights = jnp.where(causal_mask[:, :, None], jnp.exp(decay_diff), 0.0)
        inner_wide = conv_inner.astype(jnp.float32).reshape(BLOCK_LEN, HEADS, HEAD_DIM)
        scaled = inner_wide * dt_step[:, :, None]
        mixed_w = scores[:, :, None] * weights
        y_intra = jnp.einsum('tsh,shp->thp', mixed_w, scaled, precision=lax.Precision.HIGHEST)
        c_wide = c_mat.astype(jnp.float32)
        b_wide = b_mat.astype(jnp.float32)
        y_inter = jnp.exp(cum_decay)[:, :, None] * jnp.einsum('tn,hpn->thp', c_wide, state, precision=lax.Precision.HIGHEST)
        ssm_out = y_intra + y_inter + d_skip[None, :, None] * inner_wide
        block_last = cum_decay[-1]
        tail_decay = jnp.exp(block_last[None, :] - cum_decay)
        fresh = jnp.einsum('sh,shp,sn->hpn', tail_decay, scaled, b_wide, precision=lax.Precision.HIGHEST)
        new_state = jnp.exp(block_last)[:, None, None] * state + fresh
        gated = ssm_out.reshape(BLOCK_LEN, channels) * jax.nn.silu(gate_z)
        scaled_out = (gated * lax.rsqrt(lax.optimization_barrier(jnp.mean(gated * gated, axis=-1, keepdims=True)) + EPS) * ssm_gain).astype(jnp.bfloat16)
        mixer = split_sum(scaled_out, w_out)
        resid = (block_tokens.astype(jnp.float32) + mixer).astype(jnp.bfloat16)
        mlp_in = rms_rows(resid, norm2_gain).astype(jnp.bfloat16)
        mlp_gate = jnp.dot(mlp_in, w_gate, preferred_element_type=jnp.float32)
        mlp_up = jnp.dot(mlp_in, w_up, preferred_element_type=jnp.float32)
        hidden = (jax.nn.silu(mlp_gate) * mlp_up).astype(jnp.bfloat16)
        mlp_down = split_sum(hidden, w_down)
        layer_out = (resid.astype(jnp.float32) + mlp_down).astype(jnp.bfloat16)
        return ((new_state, inner_rows[-3:], bc_rows[-3:]), layer_out)
    start_state = jnp.zeros((HEADS, HEAD_DIM, STATE_DIM), jnp.float32)
    start_inner = jnp.zeros((3, channels), jnp.bfloat16)
    start_bc = jnp.zeros((3, 2 * STATE_DIM), jnp.bfloat16)
    blocks = tokens.reshape(block_count, BLOCK_LEN, WIDTH)
    final_carry, outputs = lax.scan(block_step, (start_state, start_inner, start_bc), blocks)
    return outputs.reshape(SEQ_LEN, WIDTH)
```

```python
import jax
import jax.numpy as jnp
from jax import lax
from jax.sharding import PartitionSpec as P

HEADS = 80
HEAD_DIM = 64
STATE_DIM = 128
BLOCK_LEN = 256


EPS = 1e-05


def from_behind(value, axis, steps):
    count = lax.axis_size(axis)
    first, last = (max(0, -steps), min(count, count - steps))
    return lax.ppermute(value, axis, [(source, source + steps) for source in range(first, last)])


def shifted(value, axis, steps):
    count = lax.axis_size(axis)
    return lax.ppermute(value, axis, [(source, source + steps) for source in range(count - steps)])


def join_packed(prior, later):
    head_dim = later.shape[1] - 1
    later_log = later[:, head_dim:, :]
    total_log = prior[:, head_dim:, :] + later_log
    state = later[:, :head_dim, :] + jnp.exp(later_log) * prior[:, :head_dim, :]
    return jnp.concatenate([state, total_log], axis=1)


def exclusive_prefix(packed, axis):
    count = lax.axis_size(axis)
    before = jnp.zeros_like(packed)
    upto = packed
    stride = 1
    while stride < count:
        parts = [shifted(upto, axis, k * stride) for k in (3, 2, 1) if k * stride < count]
        older = parts[0]
        for part in parts[1:]:
            older = join_packed(older, part)
        before = join_packed(older, before)
        upto = join_packed(older, upto)
        stride *= 4
    return before


def rms_rows(values, gain):
    wide = values.astype(jnp.float32)
    return wide * lax.rsqrt(jnp.mean(wide * wide, axis=-1, keepdims=True) + EPS) * gain


def conv_four(rim, current, kernel):
    extended = jnp.concatenate([rim, current], axis=0).astype(jnp.float32)
    length = current.shape[0]
    result = kernel[0] * extended[0:length]
    for offset in range(1, 4):
        result = result + kernel[offset] * extended[offset : offset + length]
    return result


def carry_step(state, pieces):
    decay_now, fresh = pieces
    return (decay_now[:, None, None] * state + fresh, state)


def local(
    tokens,
    norm1_gain,
    w_z,
    w_x,
    w_bc,
    w_dt,
    dt_bias,
    a_log,
    conv_x,
    conv_bc,
    d_skip,
    ssm_gain,
    w_out,
    norm2_gain,
    w_gate,
    w_up,
    w_down,
):
    gathered = lax.all_gather(tokens, "tp", axis=0, tiled=True)
    normed = rms_rows(gathered, norm1_gain).astype(jnp.bfloat16)
    bc_rows = jnp.dot(normed, w_bc, preferred_element_type=jnp.float32).astype(jnp.bfloat16)
    group_len = gathered.shape[0]
    head_count = w_dt.shape[1]
    channels = w_x.shape[1]
    gate_z = jnp.dot(normed, w_z, preferred_element_type=jnp.float32)
    inner_rows = jnp.dot(normed, w_x, preferred_element_type=jnp.float32).astype(jnp.bfloat16)
    dt_raw = jnp.dot(normed, w_dt, preferred_element_type=jnp.float32)
    rims = from_behind(jnp.concatenate([inner_rows[-3:], bc_rows[-3:]], axis=1), "ctx", 1)
    rim_inner, rim_bc = rims[:, :channels], rims[:, channels:]
    conv_inner = jax.nn.silu(conv_four(rim_inner, inner_rows, conv_x)).astype(jnp.bfloat16)
    conv_bcm = jax.nn.silu(conv_four(rim_bc, bc_rows, conv_bc)).astype(jnp.bfloat16)
    dt_step = jax.nn.softplus(dt_raw + dt_bias)
    log_decay = -dt_step * jnp.exp(a_log)
    block_count = group_len // BLOCK_LEN
    log_blocks = log_decay.reshape(block_count, BLOCK_LEN, head_count)
    step_blocks = dt_step.reshape(block_count, BLOCK_LEN, head_count)
    cum_decay = jnp.cumsum(log_blocks, axis=1)
    b_mat = conv_bcm[:, :STATE_DIM].reshape(block_count, BLOCK_LEN, STATE_DIM)
    c_mat = conv_bcm[:, STATE_DIM:].reshape(block_count, BLOCK_LEN, STATE_DIM)
    scores = jnp.einsum("btn,bsn->bts", c_mat, b_mat, preferred_element_type=jnp.float32)
    causal_mask = jnp.tril(jnp.ones((BLOCK_LEN, BLOCK_LEN), dtype=bool))[None, :, :, None]
    decay_diff = jnp.where(causal_mask, cum_decay[:, :, None, :] - cum_decay[:, None, :, :], 0.0)
    weights = jnp.where(causal_mask, jnp.exp(decay_diff), 0.0)
    inner_wide = conv_inner.astype(jnp.float32).reshape(
        block_count, BLOCK_LEN, head_count, HEAD_DIM
    )
    scaled = inner_wide * step_blocks[..., None]
    mixed_w = scores[..., None] * weights
    y_intra = jnp.einsum("btsh,bshp->bthp", mixed_w, scaled, precision=lax.Precision.HIGHEST)
    block_last = cum_decay[:, -1, :]
    tail_decay = jnp.exp(block_last[:, None, :] - cum_decay)
    b_wide = b_mat.astype(jnp.float32)
    c_wide = c_mat.astype(jnp.float32)
    block_states = jnp.einsum(
        "bsh,bshp,bsn->bhpn", tail_decay, scaled, b_wide, precision=lax.Precision.HIGHEST
    )
    block_decay = jnp.exp(block_last)
    zero_state = jnp.zeros((head_count, HEAD_DIM, STATE_DIM), jnp.float32)
    local_final, local_in = lax.scan(carry_step, zero_state, (block_decay, block_states))
    total_log = jnp.sum(block_last, axis=0)
    prior_decay = jnp.exp(jnp.cumsum(block_last, axis=0) - block_last)
    packed = jnp.concatenate(
        [local_final, jnp.broadcast_to(total_log[:, None, None], (head_count, 1, STATE_DIM))], axis=1
    )
    incoming = exclusive_prefix(packed, "ctx")[:, :HEAD_DIM, :]
    state_in = local_in + prior_decay[:, :, None, None] * incoming[None]
    y_inter = jnp.exp(cum_decay)[..., None] * jnp.einsum(
        "btn,bhpn->bthp", c_wide, state_in, precision=lax.Precision.HIGHEST
    )
    ssm_out = y_intra + y_inter + d_skip[None, None, :, None] * inner_wide
    gated = ssm_out.reshape(group_len, channels) * jax.nn.silu(gate_z)
    squares = jnp.sum(gated * gated, axis=-1)
    squares_hi = squares.astype(jnp.bfloat16)
    squares_lo = (squares - squares_hi.astype(jnp.float32)).astype(jnp.bfloat16)
    extra = jnp.zeros((group_len, 128), jnp.bfloat16)
    extra = extra.at[:, 0].set(squares_hi).at[:, 1].set(squares_lo)
    piece = (gated * ssm_gain).astype(jnp.bfloat16)
    product = jnp.dot(piece, w_out, preferred_element_type=jnp.float32).astype(jnp.bfloat16)
    reduced = lax.psum_scatter(
        jnp.concatenate([product, extra], axis=1), "tp", scatter_dimension=0, tiled=True
    )
    width = w_out.shape[1]
    squares_own = reduced[:, width].astype(jnp.float32) + reduced[:, width + 1].astype(jnp.float32)
    scale = lax.rsqrt(squares_own / (HEADS * HEAD_DIM) + EPS)
    mixer_own = reduced[:, :width].astype(jnp.float32) * scale[:, None]
    resid = (tokens.astype(jnp.float32) + mixer_own).astype(jnp.bfloat16)
    normed_own = rms_rows(resid, norm2_gain).astype(jnp.bfloat16)
    mlp_in = lax.all_gather(normed_own, "tp", axis=0, tiled=True)
    mlp_gate = jnp.dot(mlp_in, w_gate, preferred_element_type=jnp.float32)
    mlp_up = jnp.dot(mlp_in, w_up, preferred_element_type=jnp.float32)
    hidden = (jax.nn.silu(mlp_gate) * mlp_up).astype(jnp.bfloat16)
    piece = hidden
    mlp_down = lax.psum_scatter(
        jnp.dot(piece, w_down, preferred_element_type=jnp.float32).astype(jnp.bfloat16),
        "tp",
        scatter_dimension=0,
        tiled=True,
    ).astype(jnp.float32)
    return (resid.astype(jnp.float32) + mlp_down).astype(jnp.bfloat16)


def solution(mesh):
    return jax.shard_map(
        local,
        mesh=mesh,
        in_specs=(
            P(("ctx", "tp"), None),
            P(),
            P(None, "tp"),
            P(None, "tp"),
            P(),
            P(None, "tp"),
            P("tp"),
            P("tp"),
            P(None, "tp"),
            P(),
            P("tp"),
            P("tp"),
            P("tp", None),
            P(),
            P(None, "tp"),
            P(None, "tp"),
            P("tp", None),
        ),
        out_specs=P(("ctx", "tp"), None),
        check_vma=False,
    )
```

```python
import jax
import jax.numpy as jnp
from jax import lax
from jax.sharding import PartitionSpec as P

HEADS = 80
HEAD_DIM = 64
STATE_DIM = 128
BLOCK_LEN = 256


EPS = 1e-05


def from_behind(value, axis, steps):
    count = lax.axis_size(axis)
    first, last = (max(0, -steps), min(count, count - steps))
    return lax.ppermute(value, axis, [(source, source + steps) for source in range(first, last)])


def shifted(value, axis, steps):
    count = lax.axis_size(axis)
    return lax.ppermute(value, axis, [(source, source + steps) for source in range(count - steps)])


def join_packed(prior, later):
    head_dim = later.shape[1] - 1
    later_log = later[:, head_dim:, :]
    total_log = prior[:, head_dim:, :] + later_log
    state = later[:, :head_dim, :] + jnp.exp(later_log) * prior[:, :head_dim, :]
    return jnp.concatenate([state, total_log], axis=1)


def exclusive_prefix(packed, axis):
    count = lax.axis_size(axis)
    before = jnp.zeros_like(packed)
    upto = packed
    stride = 1
    while stride < count:
        parts = [shifted(upto, axis, k * stride) for k in (3, 2, 1) if k * stride < count]
        older = parts[0]
        for part in parts[1:]:
            older = join_packed(older, part)
        before = join_packed(older, before)
        upto = join_packed(older, upto)
        stride *= 4
    return before


def gather_group(rows):
    across = lax.all_gather(rows, "z", axis=0)
    both = lax.all_gather(across, "core", axis=0)
    return jnp.swapaxes(both, 0, 1).reshape((-1,) + rows.shape[1:])


def scatter_group(rows):
    chips = lax.axis_size("z")
    cores = lax.axis_size("core")
    blocks = rows.reshape((chips, cores, -1) + rows.shape[1:])
    blocks = jnp.swapaxes(blocks, 0, 1)
    on_chip = lax.psum_scatter(blocks, "core", scatter_dimension=0)
    return lax.psum_scatter(on_chip, "z", scatter_dimension=0)


def rms_rows(values, gain):
    wide = values.astype(jnp.float32)
    return wide * lax.rsqrt(jnp.mean(wide * wide, axis=-1, keepdims=True) + EPS) * gain


def conv_four(rim, current, kernel):
    extended = jnp.concatenate([rim, current], axis=0).astype(jnp.float32)
    length = current.shape[0]
    result = kernel[0] * extended[0:length]
    for offset in range(1, 4):
        result = result + kernel[offset] * extended[offset : offset + length]
    return result


def carry_step(state, pieces):
    decay_now, fresh = pieces
    return (decay_now[:, None, None] * state + fresh, state)


def local(
    tokens,
    norm1_gain,
    w_z,
    w_x,
    w_bc,
    w_dt,
    dt_bias,
    a_log,
    conv_x,
    conv_bc,
    d_skip,
    ssm_gain,
    w_out,
    norm2_gain,
    w_gate,
    w_up,
    w_down,
):
    gathered = gather_group(tokens)
    normed = rms_rows(gathered, norm1_gain).astype(jnp.bfloat16)
    bc_rows = jnp.dot(normed, w_bc, preferred_element_type=jnp.float32).astype(jnp.bfloat16)
    group_len = gathered.shape[0]
    head_count = w_dt.shape[1]
    channels = w_x.shape[1]
    gate_z = jnp.dot(normed, w_z, preferred_element_type=jnp.float32)
    inner_rows = jnp.dot(normed, w_x, preferred_element_type=jnp.float32).astype(jnp.bfloat16)
    dt_raw = jnp.dot(normed, w_dt, preferred_element_type=jnp.float32)
    rims = from_behind(jnp.concatenate([inner_rows[-3:], bc_rows[-3:]], axis=1), "ctx", 1)
    rim_inner, rim_bc = rims[:, :channels], rims[:, channels:]
    conv_inner = jax.nn.silu(conv_four(rim_inner, inner_rows, conv_x)).astype(jnp.bfloat16)
    conv_bcm = jax.nn.silu(conv_four(rim_bc, bc_rows, conv_bc)).astype(jnp.bfloat16)
    dt_step = jax.nn.softplus(dt_raw + dt_bias)
    log_decay = -dt_step * jnp.exp(a_log)
    block_count = group_len // BLOCK_LEN
    log_blocks = log_decay.reshape(block_count, BLOCK_LEN, head_count)
    step_blocks = dt_step.reshape(block_count, BLOCK_LEN, head_count)
    cum_decay = jnp.cumsum(log_blocks, axis=1)
    b_mat = conv_bcm[:, :STATE_DIM].reshape(block_count, BLOCK_LEN, STATE_DIM)
    c_mat = conv_bcm[:, STATE_DIM:].reshape(block_count, BLOCK_LEN, STATE_DIM)
    scores = jnp.einsum("btn,bsn->bts", c_mat, b_mat, preferred_element_type=jnp.float32)
    causal_mask = jnp.tril(jnp.ones((BLOCK_LEN, BLOCK_LEN), dtype=bool))[None, :, :, None]
    decay_diff = jnp.where(causal_mask, cum_decay[:, :, None, :] - cum_decay[:, None, :, :], 0.0)
    weights = jnp.where(causal_mask, jnp.exp(decay_diff), 0.0)
    inner_wide = conv_inner.astype(jnp.float32).reshape(
        block_count, BLOCK_LEN, head_count, HEAD_DIM
    )
    scaled = inner_wide * step_blocks[..., None]
    mixed_w = scores[..., None] * weights
    y_intra = jnp.einsum("btsh,bshp->bthp", mixed_w, scaled, precision=lax.Precision.HIGHEST)
    block_last = cum_decay[:, -1, :]
    tail_decay = jnp.exp(block_last[:, None, :] - cum_decay)
    b_wide = b_mat.astype(jnp.float32)
    c_wide = c_mat.astype(jnp.float32)
    block_states = jnp.einsum(
        "bsh,bshp,bsn->bhpn", tail_decay, scaled, b_wide, precision=lax.Precision.HIGHEST
    )
    block_decay = jnp.exp(block_last)
    zero_state = jnp.zeros((head_count, HEAD_DIM, STATE_DIM), jnp.float32)
    local_final, local_in = lax.scan(carry_step, zero_state, (block_decay, block_states))
    total_log = jnp.sum(block_last, axis=0)
    prior_decay = jnp.exp(jnp.cumsum(block_last, axis=0) - block_last)
    packed = jnp.concatenate(
        [local_final, jnp.broadcast_to(total_log[:, None, None], (head_count, 1, STATE_DIM))], axis=1
    )
    incoming = exclusive_prefix(packed, "ctx")[:, :HEAD_DIM, :]
    state_in = local_in + prior_decay[:, :, None, None] * incoming[None]
    y_inter = jnp.exp(cum_decay)[..., None] * jnp.einsum(
        "btn,bhpn->bthp", c_wide, state_in, precision=lax.Precision.HIGHEST
    )
    ssm_out = y_intra + y_inter + d_skip[None, None, :, None] * inner_wide
    gated = ssm_out.reshape(group_len, channels) * jax.nn.silu(gate_z)
    squares = jnp.sum(gated * gated, axis=-1)
    squares_hi = squares.astype(jnp.bfloat16)
    squares_lo = (squares - squares_hi.astype(jnp.float32)).astype(jnp.bfloat16)
    extra = jnp.zeros((group_len, 128), jnp.bfloat16)
    extra = extra.at[:, 0].set(squares_hi).at[:, 1].set(squares_lo)
    piece = (gated * ssm_gain).astype(jnp.bfloat16)
    product = jnp.dot(piece, w_out, preferred_element_type=jnp.float32).astype(jnp.bfloat16)
    reduced = scatter_group(jnp.concatenate([product, extra], axis=1))
    width = w_out.shape[1]
    squares_own = reduced[:, width].astype(jnp.float32) + reduced[:, width + 1].astype(jnp.float32)
    scale = lax.rsqrt(squares_own / (HEADS * HEAD_DIM) + EPS)
    mixer_own = reduced[:, :width].astype(jnp.float32) * scale[:, None]
    resid = (tokens.astype(jnp.float32) + mixer_own).astype(jnp.bfloat16)
    normed_own = rms_rows(resid, norm2_gain).astype(jnp.bfloat16)
    mlp_in = gather_group(normed_own)
    mlp_gate = jnp.dot(mlp_in, w_gate, preferred_element_type=jnp.float32)
    mlp_up = jnp.dot(mlp_in, w_up, preferred_element_type=jnp.float32)
    hidden = (jax.nn.silu(mlp_gate) * mlp_up).astype(jnp.bfloat16)
    piece = hidden
    mlp_down = scatter_group(
        jnp.dot(piece, w_down, preferred_element_type=jnp.float32).astype(jnp.bfloat16)
    ).astype(jnp.float32)
    return (resid.astype(jnp.float32) + mlp_down).astype(jnp.bfloat16)


def solution(mesh):
    cores = 2
    devices = mesh.devices.reshape(mesh.shape["ctx"], mesh.shape["tp"] // cores, cores)
    split = jax.sharding.Mesh(devices, ("ctx", "z", "core"))
    return jax.shard_map(
        local,
        mesh=split,
        in_specs=(
            P(("ctx", "z", "core"), None),
            P(),
            P(None, ("z", "core")),
            P(None, ("z", "core")),
            P(),
            P(None, ("z", "core")),
            P(("z", "core")),
            P(("z", "core")),
            P(None, ("z", "core")),
            P(),
            P(("z", "core")),
            P(("z", "core")),
            P(("z", "core"), None),
            P(),
            P(None, ("z", "core")),
            P(None, ("z", "core")),
            P(("z", "core"), None),
        ),
        out_specs=P(("ctx", "z", "core"), None),
        check_vma=False,
    )
```

```python
import jax
import jax.numpy as jnp
from jax import lax
from jax.sharding import PartitionSpec as P

HEADS = 80
HEAD_DIM = 64
STATE_DIM = 128
BLOCK_LEN = 256


EPS = 1e-05


def from_behind(value, axis, steps):
    count = lax.axis_size(axis)
    first, last = (max(0, -steps), min(count, count - steps))
    return lax.ppermute(value, axis, [(source, source + steps) for source in range(first, last)])


def shifted(value, axis, steps):
    count = lax.axis_size(axis)
    return lax.ppermute(value, axis, [(source, source + steps) for source in range(count - steps)])


def join_packed(prior, later):
    head_dim = later.shape[1] - 1
    later_log = later[:, head_dim:, :]
    total_log = prior[:, head_dim:, :] + later_log
    state = later[:, :head_dim, :] + jnp.exp(later_log) * prior[:, :head_dim, :]
    return jnp.concatenate([state, total_log], axis=1)


def exclusive_prefix(packed, axis):
    count = lax.axis_size(axis)
    before = jnp.zeros_like(packed)
    upto = packed
    stride = 1
    while stride < count:
        parts = [shifted(upto, axis, k * stride) for k in (3, 2, 1) if k * stride < count]
        older = parts[0]
        for part in parts[1:]:
            older = join_packed(older, part)
        before = join_packed(older, before)
        upto = join_packed(older, upto)
        stride *= 4
    return before


def rms_rows(values, gain):
    wide = values.astype(jnp.float32)
    return wide * lax.rsqrt(jnp.mean(wide * wide, axis=-1, keepdims=True) + EPS) * gain


def conv_four(rim, current, kernel):
    extended = jnp.concatenate([rim, current], axis=0).astype(jnp.float32)
    length = current.shape[0]
    result = kernel[0] * extended[0:length]
    for offset in range(1, 4):
        result = result + kernel[offset] * extended[offset : offset + length]
    return result


def local(
    tokens,
    norm1_gain,
    w_z,
    w_x,
    w_bc,
    w_dt,
    dt_bias,
    a_log,
    conv_x,
    conv_bc,
    d_skip,
    ssm_gain,
    w_out,
    norm2_gain,
    w_gate,
    w_up,
    w_down,
):
    gathered = lax.all_gather(tokens, "tp", axis=0, tiled=True)
    normed = rms_rows(gathered, norm1_gain).astype(jnp.bfloat16)
    bc_rows = jnp.dot(normed, w_bc, preferred_element_type=jnp.float32).astype(jnp.bfloat16)
    group_len = gathered.shape[0]
    head_count = w_dt.shape[1]
    channels = w_x.shape[1]
    gate_z = jnp.dot(normed, w_z, preferred_element_type=jnp.float32)
    inner_rows = jnp.dot(normed, w_x, preferred_element_type=jnp.float32).astype(jnp.bfloat16)
    dt_raw = jnp.dot(normed, w_dt, preferred_element_type=jnp.float32)
    rims = from_behind(jnp.concatenate([inner_rows[-3:], bc_rows[-3:]], axis=1), "ctx", 1)
    rim_inner, rim_bc = rims[:, :channels], rims[:, channels:]
    conv_inner = jax.nn.silu(conv_four(rim_inner, inner_rows, conv_x)).astype(jnp.bfloat16)
    conv_bcm = jax.nn.silu(conv_four(rim_bc, bc_rows, conv_bc)).astype(jnp.bfloat16)
    dt_step = jax.nn.softplus(dt_raw + dt_bias)
    log_decay = -dt_step * jnp.exp(a_log)
    block_count = group_len // BLOCK_LEN
    log_blocks = log_decay.reshape(block_count, BLOCK_LEN, head_count)
    step_blocks = dt_step.reshape(block_count, BLOCK_LEN, head_count)
    lower = jnp.tril(jnp.ones((BLOCK_LEN, BLOCK_LEN), jnp.float32))
    cum_decay = jnp.einsum("ts,bsh->bth", lower, log_blocks, precision=lax.Precision.HIGHEST)
    b_mat = conv_bcm[:, :STATE_DIM].reshape(block_count, BLOCK_LEN, STATE_DIM)
    c_mat = conv_bcm[:, STATE_DIM:].reshape(block_count, BLOCK_LEN, STATE_DIM)
    scores = jnp.einsum("btn,bsn->bts", c_mat, b_mat, preferred_element_type=jnp.float32)
    causal_mask = jnp.tril(jnp.ones((BLOCK_LEN, BLOCK_LEN), dtype=bool))[None, :, :, None]
    decay_diff = jnp.where(causal_mask, cum_decay[:, :, None, :] - cum_decay[:, None, :, :], 0.0)
    weights = jnp.where(causal_mask, jnp.exp(decay_diff), 0.0)
    inner_wide = conv_inner.astype(jnp.float32).reshape(
        block_count, BLOCK_LEN, head_count, HEAD_DIM
    )
    scaled = inner_wide * step_blocks[..., None]
    mixed_w = scores[..., None] * weights
    y_intra = jnp.einsum("btsh,bshp->bthp", mixed_w, scaled, precision=lax.Precision.HIGHEST)
    block_last = cum_decay[:, -1, :]
    tail_decay = jnp.exp(block_last[:, None, :] - cum_decay)
    b_wide = b_mat.astype(jnp.float32)
    c_wide = c_mat.astype(jnp.float32)
    block_states = jnp.einsum(
        "bsh,bshp,bsn->bhpn", tail_decay, scaled, b_wide, precision=lax.Precision.HIGHEST
    )
    block_decay = jnp.exp(block_last)
    zero_state = jnp.zeros((head_count, HEAD_DIM, STATE_DIM), jnp.float32)
    running = zero_state
    entering = []
    for block in range(block_count):
        entering.append(running)
        running = block_decay[block][:, None, None] * running + block_states[block]
    local_final, local_in = running, jnp.stack(entering)
    total_log = jnp.sum(block_last, axis=0)
    prior_decay = jnp.exp(jnp.cumsum(block_last, axis=0) - block_last)
    packed = jnp.concatenate(
        [local_final, jnp.broadcast_to(total_log[:, None, None], (head_count, 1, STATE_DIM))], axis=1
    )
    incoming = exclusive_prefix(packed, "ctx")[:, :HEAD_DIM, :]
    state_in = local_in + prior_decay[:, :, None, None] * incoming[None]
    y_inter = jnp.exp(cum_decay)[..., None] * jnp.einsum(
        "btn,bhpn->bthp", c_wide, state_in, precision=lax.Precision.HIGHEST
    )
    ssm_out = y_intra + y_inter + d_skip[None, None, :, None] * inner_wide
    gated = ssm_out.reshape(group_len, channels) * jax.nn.silu(gate_z)
    squares = jnp.sum(gated * gated, axis=-1)
    squares_hi = squares.astype(jnp.bfloat16)
    squares_lo = (squares - squares_hi.astype(jnp.float32)).astype(jnp.bfloat16)
    extra = jnp.zeros((group_len, 128), jnp.bfloat16)
    extra = extra.at[:, 0].set(squares_hi).at[:, 1].set(squares_lo)
    piece = (gated * ssm_gain).astype(jnp.bfloat16)
    product = jnp.dot(piece, w_out, preferred_element_type=jnp.float32).astype(jnp.bfloat16)
    reduced = lax.psum(jnp.concatenate([product, extra], axis=1), "tp")
    width = w_out.shape[1]
    squares_all = reduced[:, width].astype(jnp.float32) + reduced[:, width + 1].astype(jnp.float32)
    scale = lax.rsqrt(squares_all / (HEADS * HEAD_DIM) + EPS)
    mixer_all = reduced[:, :width].astype(jnp.float32) * scale[:, None]
    resid_all = (gathered.astype(jnp.float32) + mixer_all).astype(jnp.bfloat16)
    mlp_in = rms_rows(resid_all, norm2_gain).astype(jnp.bfloat16)
    own_rows = tokens.shape[0]
    resid = lax.dynamic_slice_in_dim(resid_all, lax.axis_index("tp") * own_rows, own_rows, 0)
    mlp_gate = jnp.dot(mlp_in, w_gate, preferred_element_type=jnp.float32)
    mlp_up = jnp.dot(mlp_in, w_up, preferred_element_type=jnp.float32)
    hidden = (jax.nn.silu(mlp_gate) * mlp_up).astype(jnp.bfloat16)
    piece = hidden
    mlp_down = lax.psum_scatter(
        jnp.dot(piece, w_down, preferred_element_type=jnp.float32).astype(jnp.bfloat16),
        "tp",
        scatter_dimension=0,
        tiled=True,
    ).astype(jnp.float32)
    return (resid.astype(jnp.float32) + mlp_down).astype(jnp.bfloat16)


def solution(mesh):
    return jax.shard_map(
        local,
        mesh=mesh,
        in_specs=(
            P(("ctx", "tp"), None),
            P(),
            P(None, "tp"),
            P(None, "tp"),
            P(),
            P(None, "tp"),
            P("tp"),
            P("tp"),
            P(None, "tp"),
            P(),
            P("tp"),
            P("tp"),
            P("tp", None),
            P(),
            P(None, "tp"),
            P(None, "tp"),
            P("tp", None),
        ),
        out_specs=P(("ctx", "tp"), None),
        check_vma=False,
    )
```

```python
import jax
import jax.numpy as jnp
from jax import lax
from jax.sharding import PartitionSpec as P

HEADS = 80
HEAD_DIM = 64
STATE_DIM = 128
BLOCK_LEN = 256


EPS = 1e-05


def from_behind(value, axis, steps):
    count = lax.axis_size(axis)
    first, last = (max(0, -steps), min(count, count - steps))
    return lax.ppermute(value, axis, [(source, source + steps) for source in range(first, last)])


def shifted(value, axis, steps):
    count = lax.axis_size(axis)
    return lax.ppermute(value, axis, [(source, source + steps) for source in range(count - steps)])


def join_packed(prior, later):
    head_dim = later.shape[1] - 1
    later_log = later[:, head_dim:, :]
    total_log = prior[:, head_dim:, :] + later_log
    state = later[:, :head_dim, :] + jnp.exp(later_log) * prior[:, :head_dim, :]
    return jnp.concatenate([state, total_log], axis=1)


def exclusive_prefix(packed, axis):
    count = lax.axis_size(axis)
    before = jnp.zeros_like(packed)
    upto = packed
    stride = 1
    while stride < count:
        parts = [shifted(upto, axis, k * stride) for k in (3, 2, 1) if k * stride < count]
        older = parts[0]
        for part in parts[1:]:
            older = join_packed(older, part)
        before = join_packed(older, before)
        upto = join_packed(older, upto)
        stride *= 4
    return before


def sum_partials(rows):
    count = lax.axis_size("tp")
    parts = lax.all_to_all(rows, "tp", 0, 0, tiled=True)
    parts = parts.reshape((count, -1) + rows.shape[1:]).astype(jnp.float32)
    return jnp.sum(parts, axis=0)


def rms_rows(values, gain):
    wide = values.astype(jnp.float32)
    return wide * lax.rsqrt(jnp.mean(wide * wide, axis=-1, keepdims=True) + EPS) * gain


def conv_four(rim, current, kernel):
    extended = jnp.concatenate([rim, current], axis=0).astype(jnp.float32)
    length = current.shape[0]
    result = kernel[0] * extended[0:length]
    for offset in range(1, 4):
        result = result + kernel[offset] * extended[offset : offset + length]
    return result


def local(
    tokens,
    norm1_gain,
    w_z,
    w_x,
    w_bc,
    w_dt,
    dt_bias,
    a_log,
    conv_x,
    conv_bc,
    d_skip,
    ssm_gain,
    w_out,
    norm2_gain,
    w_gate,
    w_up,
    w_down,
):
    gathered = lax.all_gather(tokens, "tp", axis=0, tiled=True)
    normed = rms_rows(gathered, norm1_gain).astype(jnp.bfloat16)
    bc_rows = jnp.dot(normed, w_bc, preferred_element_type=jnp.float32).astype(jnp.bfloat16)
    group_len = gathered.shape[0]
    head_count = w_dt.shape[1]
    channels = w_x.shape[1]
    gate_z = jnp.dot(normed, w_z, preferred_element_type=jnp.float32)
    inner_rows = jnp.dot(normed, w_x, preferred_element_type=jnp.float32).astype(jnp.bfloat16)
    dt_raw = jnp.dot(normed, w_dt, preferred_element_type=jnp.float32)
    rims = from_behind(jnp.concatenate([inner_rows[-3:], bc_rows[-3:]], axis=1), "ctx", 1)
    rim_inner, rim_bc = rims[:, :channels], rims[:, channels:]
    conv_inner = jax.nn.silu(conv_four(rim_inner, inner_rows, conv_x)).astype(jnp.bfloat16)
    conv_bcm = jax.nn.silu(conv_four(rim_bc, bc_rows, conv_bc)).astype(jnp.bfloat16)
    dt_step = jax.nn.softplus(dt_raw + dt_bias)
    log_decay = -dt_step * jnp.exp(a_log)
    block_count = group_len // BLOCK_LEN
    log_blocks = log_decay.reshape(block_count, BLOCK_LEN, head_count)
    step_blocks = dt_step.reshape(block_count, BLOCK_LEN, head_count)
    lower = jnp.tril(jnp.ones((BLOCK_LEN, BLOCK_LEN), jnp.float32))
    cum_decay = jnp.einsum("ts,bsh->bth", lower, log_blocks, precision=lax.Precision.HIGHEST)
    b_mat = conv_bcm[:, :STATE_DIM].reshape(block_count, BLOCK_LEN, STATE_DIM)
    c_mat = conv_bcm[:, STATE_DIM:].reshape(block_count, BLOCK_LEN, STATE_DIM)
    scores = jnp.einsum("btn,bsn->bts", c_mat, b_mat, preferred_element_type=jnp.float32)
    causal_mask = jnp.tril(jnp.ones((BLOCK_LEN, BLOCK_LEN), dtype=bool))[None, :, :, None]
    decay_diff = jnp.where(causal_mask, cum_decay[:, :, None, :] - cum_decay[:, None, :, :], 0.0)
    weights = jnp.where(causal_mask, jnp.exp(decay_diff), 0.0)
    inner_wide = conv_inner.astype(jnp.float32).reshape(
        block_count, BLOCK_LEN, head_count, HEAD_DIM
    )
    scaled = inner_wide * step_blocks[..., None]
    mixed_w = scores[..., None] * weights
    y_intra = jnp.einsum("btsh,bshp->bthp", mixed_w, scaled, precision=lax.Precision.HIGHEST)
    block_last = cum_decay[:, -1, :]
    tail_decay = jnp.exp(block_last[:, None, :] - cum_decay)
    b_wide = b_mat.astype(jnp.float32)
    c_wide = c_mat.astype(jnp.float32)
    block_states = jnp.einsum(
        "bsh,bshp,bsn->bhpn", tail_decay, scaled, b_wide, precision=lax.Precision.HIGHEST
    )
    block_decay = jnp.exp(block_last)
    zero_state = jnp.zeros((head_count, HEAD_DIM, STATE_DIM), jnp.float32)
    running = zero_state
    entering = []
    for block in range(block_count):
        entering.append(running)
        running = block_decay[block][:, None, None] * running + block_states[block]
    local_final, local_in = running, jnp.stack(entering)
    total_log = jnp.sum(block_last, axis=0)
    prior_decay = jnp.exp(jnp.cumsum(block_last, axis=0) - block_last)
    packed = jnp.concatenate(
        [local_final, jnp.broadcast_to(total_log[:, None, None], (head_count, 1, STATE_DIM))], axis=1
    )
    incoming = exclusive_prefix(packed, "ctx")[:, :HEAD_DIM, :]
    state_in = local_in + prior_decay[:, :, None, None] * incoming[None]
    y_inter = jnp.exp(cum_decay)[..., None] * jnp.einsum(
        "btn,bhpn->bthp", c_wide, state_in, precision=lax.Precision.HIGHEST
    )
    ssm_out = y_intra + y_inter + d_skip[None, None, :, None] * inner_wide
    gated = ssm_out.reshape(group_len, channels) * jax.nn.silu(gate_z)
    squares = jnp.sum(gated * gated, axis=-1)
    squares_hi = squares.astype(jnp.bfloat16)
    squares_lo = (squares - squares_hi.astype(jnp.float32)).astype(jnp.bfloat16)
    extra = jnp.zeros((group_len, 128), jnp.bfloat16)
    extra = extra.at[:, 0].set(squares_hi).at[:, 1].set(squares_lo)
    piece = (gated * ssm_gain).astype(jnp.bfloat16)
    product = jnp.dot(piece, w_out, preferred_element_type=jnp.float32).astype(jnp.bfloat16)
    reduced = sum_partials(jnp.concatenate([product, extra], axis=1))
    width = w_out.shape[1]
    squares_own = reduced[:, width] + reduced[:, width + 1]
    scale = lax.rsqrt(squares_own / (HEADS * HEAD_DIM) + EPS)
    mixer_own = reduced[:, :width] * scale[:, None]
    resid = (tokens.astype(jnp.float32) + mixer_own).astype(jnp.bfloat16)
    normed_own = rms_rows(resid, norm2_gain).astype(jnp.bfloat16)
    mlp_in = lax.all_gather(normed_own, "tp", axis=0, tiled=True)
    mlp_gate = jnp.dot(mlp_in, w_gate, preferred_element_type=jnp.float32)
    mlp_up = jnp.dot(mlp_in, w_up, preferred_element_type=jnp.float32)
    hidden = (jax.nn.silu(mlp_gate) * mlp_up).astype(jnp.bfloat16)
    piece = hidden
    mlp_down = sum_partials(
        jnp.dot(piece, w_down, preferred_element_type=jnp.float32).astype(jnp.bfloat16)
    )
    return (resid.astype(jnp.float32) + mlp_down).astype(jnp.bfloat16)


def solution(mesh):
    return jax.shard_map(
        local,
        mesh=mesh,
        in_specs=(
            P(("ctx", "tp"), None),
            P(),
            P(None, "tp"),
            P(None, "tp"),
            P(),
            P(None, "tp"),
            P("tp"),
            P("tp"),
            P(None, "tp"),
            P(),
            P("tp"),
            P("tp"),
            P("tp", None),
            P(),
            P(None, "tp"),
            P(None, "tp"),
            P("tp", None),
        ),
        out_specs=P(("ctx", "tp"), None),
        check_vma=False,
    )
```

```python
import jax
import jax.numpy as jnp
from jax import lax
from jax.sharding import PartitionSpec as P

HEADS = 80
HEAD_DIM = 64
STATE_DIM = 128
BLOCK_LEN = 256


EPS = 1e-05


def from_behind(value, axis, steps):
    count = lax.axis_size(axis)
    first, last = (max(0, -steps), min(count, count - steps))
    return lax.ppermute(value, axis, [(source, source + steps) for source in range(first, last)])


def shifted(value, axis, steps):
    count = lax.axis_size(axis)
    return lax.ppermute(value, axis, [(source, source + steps) for source in range(count - steps)])


def join_packed(prior, later):
    head_dim = later.shape[1] - 1
    later_log = later[:, head_dim:, :]
    total_log = prior[:, head_dim:, :] + later_log
    state = later[:, :head_dim, :] + jnp.exp(later_log) * prior[:, :head_dim, :]
    return jnp.concatenate([state, total_log], axis=1)


def exclusive_prefix(packed, axis):
    count = lax.axis_size(axis)
    before = jnp.zeros_like(packed)
    upto = packed
    stride = 1
    while stride < count:
        parts = [shifted(upto, axis, k * stride) for k in (3, 2, 1) if k * stride < count]
        older = parts[0]
        for part in parts[1:]:
            older = join_packed(older, part)
        before = join_packed(older, before)
        upto = join_packed(older, upto)
        stride *= 4
    return before


def rms_rows(values, gain):
    wide = values.astype(jnp.float32)
    return wide * lax.rsqrt(jnp.mean(wide * wide, axis=-1, keepdims=True) + EPS) * gain


def conv_four(rim, current, kernel):
    extended = jnp.concatenate([rim, current], axis=0).astype(jnp.float32)
    length = current.shape[0]
    result = kernel[0] * extended[0:length]
    for offset in range(1, 4):
        result = result + kernel[offset] * extended[offset : offset + length]
    return result


def local(
    tokens,
    norm1_gain,
    w_z,
    w_x,
    w_bc,
    w_dt,
    dt_bias,
    a_log,
    conv_x,
    conv_bc,
    d_skip,
    ssm_gain,
    w_out,
    norm2_gain,
    w_gate,
    w_up,
    w_down,
):
    gathered = lax.all_gather(tokens, "tp", axis=0, tiled=True)
    normed = rms_rows(gathered, norm1_gain).astype(jnp.bfloat16)
    bc_rows = jnp.dot(normed, w_bc, preferred_element_type=jnp.float32).astype(jnp.bfloat16)
    group_len = gathered.shape[0]
    head_count = w_dt.shape[1]
    channels = w_x.shape[1]
    gate_z = jnp.dot(normed, w_z, preferred_element_type=jnp.float32)
    inner_rows = jnp.dot(normed, w_x, preferred_element_type=jnp.float32).astype(jnp.bfloat16)
    dt_raw = jnp.dot(normed, w_dt, preferred_element_type=jnp.float32)
    rims = from_behind(jnp.concatenate([inner_rows[-3:], bc_rows[-3:]], axis=1), "ctx", 1)
    rim_inner, rim_bc = rims[:, :channels], rims[:, channels:]
    conv_inner = jax.nn.silu(conv_four(rim_inner, inner_rows, conv_x)).astype(jnp.bfloat16)
    conv_bcm = jax.nn.silu(conv_four(rim_bc, bc_rows, conv_bc)).astype(jnp.bfloat16)
    dt_step = jax.nn.softplus(dt_raw + dt_bias)
    log_decay = -dt_step * jnp.exp(a_log)
    block_count = group_len // BLOCK_LEN
    log_blocks = log_decay.reshape(block_count, BLOCK_LEN, head_count)
    step_blocks = dt_step.reshape(block_count, BLOCK_LEN, head_count)
    lower = jnp.tril(jnp.ones((BLOCK_LEN, BLOCK_LEN), jnp.float32))
    cum_decay = jnp.einsum("ts,bsh->bth", lower, log_blocks, precision=lax.Precision.HIGHEST)
    b_mat = conv_bcm[:, :STATE_DIM].reshape(block_count, BLOCK_LEN, STATE_DIM)
    c_mat = conv_bcm[:, STATE_DIM:].reshape(block_count, BLOCK_LEN, STATE_DIM)
    scores = jnp.einsum("btn,bsn->bts", c_mat, b_mat, preferred_element_type=jnp.float32)
    causal_mask = jnp.tril(jnp.ones((BLOCK_LEN, BLOCK_LEN), dtype=bool))[None, :, :, None]
    decay_diff = jnp.where(causal_mask, cum_decay[:, :, None, :] - cum_decay[:, None, :, :], 0.0)
    weights = jnp.where(causal_mask, jnp.exp(decay_diff), 0.0)
    inner_wide = conv_inner.astype(jnp.float32).reshape(
        block_count, BLOCK_LEN, head_count, HEAD_DIM
    )
    scaled = inner_wide * step_blocks[..., None]
    mixed_w = scores[..., None] * weights
    y_intra = jnp.einsum("btsh,bshp->bthp", mixed_w, scaled, precision=lax.Precision.HIGHEST)
    block_last = cum_decay[:, -1, :]
    tail_decay = jnp.exp(block_last[:, None, :] - cum_decay)
    b_wide = b_mat.astype(jnp.float32)
    c_wide = c_mat.astype(jnp.float32)
    block_states = jnp.einsum(
        "bsh,bshp,bsn->bhpn", tail_decay, scaled, b_wide, precision=lax.Precision.HIGHEST
    )
    block_decay = jnp.exp(block_last)
    zero_state = jnp.zeros((head_count, HEAD_DIM, STATE_DIM), jnp.float32)
    running = zero_state
    entering = []
    for block in range(block_count):
        entering.append(running)
        running = block_decay[block][:, None, None] * running + block_states[block]
    local_final, local_in = running, jnp.stack(entering)
    total_log = jnp.sum(block_last, axis=0)
    prior_decay = jnp.exp(jnp.cumsum(block_last, axis=0) - block_last)
    packed = jnp.concatenate(
        [local_final, jnp.broadcast_to(total_log[:, None, None], (head_count, 1, STATE_DIM))], axis=1
    )
    incoming = exclusive_prefix(packed, "ctx")[:, :HEAD_DIM, :]
    state_in = local_in + prior_decay[:, :, None, None] * incoming[None]
    y_inter = jnp.exp(cum_decay)[..., None] * jnp.einsum(
        "btn,bhpn->bthp", c_wide, state_in, precision=lax.Precision.HIGHEST
    )
    ssm_out = y_intra + y_inter + d_skip[None, None, :, None] * inner_wide
    gated = ssm_out.reshape(group_len, channels) * jax.nn.silu(gate_z)
    squares = jnp.sum(gated * gated, axis=-1)
    squares_hi = squares.astype(jnp.bfloat16)
    squares_lo = (squares - squares_hi.astype(jnp.float32)).astype(jnp.bfloat16)
    extra = jnp.concatenate(
        [squares_hi[:, None], squares_lo[:, None], jnp.zeros((group_len, 126), jnp.bfloat16)], axis=1
    )
    piece = (gated * ssm_gain).astype(jnp.bfloat16)
    product = jnp.dot(piece, w_out, preferred_element_type=jnp.float32).astype(jnp.bfloat16)
    reduced = lax.psum_scatter(
        jnp.concatenate([product, extra], axis=1), "tp", scatter_dimension=0, tiled=True
    )
    width = w_out.shape[1]
    squares_own = reduced[:, width].astype(jnp.float32) + reduced[:, width + 1].astype(jnp.float32)
    scale = lax.rsqrt(squares_own / (HEADS * HEAD_DIM) + EPS)
    mixer_own = reduced[:, :width].astype(jnp.float32) * scale[:, None]
    resid = (tokens.astype(jnp.float32) + mixer_own).astype(jnp.bfloat16)
    normed_own = rms_rows(resid, norm2_gain).astype(jnp.bfloat16)
    mlp_in = lax.all_gather(normed_own, "tp", axis=0, tiled=True)
    mlp_gate = jnp.dot(mlp_in, w_gate, preferred_element_type=jnp.float32)
    mlp_up = jnp.dot(mlp_in, w_up, preferred_element_type=jnp.float32)
    hidden = (jax.nn.silu(mlp_gate) * mlp_up).astype(jnp.bfloat16)
    piece = hidden
    mlp_down = lax.psum_scatter(
        jnp.dot(piece, w_down, preferred_element_type=jnp.float32).astype(jnp.bfloat16),
        "tp",
        scatter_dimension=0,
        tiled=True,
    ).astype(jnp.float32)
    return (resid.astype(jnp.float32) + mlp_down).astype(jnp.bfloat16)


def solution(mesh):
    return jax.shard_map(
        local,
        mesh=mesh,
        in_specs=(
            P(("ctx", "tp"), None),
            P(),
            P(None, "tp"),
            P(None, "tp"),
            P(),
            P(None, "tp"),
            P("tp"),
            P("tp"),
            P(None, "tp"),
            P(),
            P("tp"),
            P("tp"),
            P("tp", None),
            P(),
            P(None, "tp"),
            P(None, "tp"),
            P("tp", None),
        ),
        out_specs=P(("ctx", "tp"), None),
        check_vma=False,
    )
```

```python
import jax
import jax.numpy as jnp
from jax import lax
from jax.sharding import PartitionSpec as P

HEADS = 80
HEAD_DIM = 64
STATE_DIM = 128
BLOCK_LEN = 256


EPS = 1e-05


def from_behind(value, axis, steps):
    count = lax.axis_size(axis)
    first, last = (max(0, -steps), min(count, count - steps))
    return lax.ppermute(value, axis, [(source, source + steps) for source in range(first, last)])


def shifted(value, axis, steps):
    count = lax.axis_size(axis)
    return lax.ppermute(value, axis, [(source, source + steps) for source in range(count - steps)])


def join_packed(prior, later):
    head_dim = later.shape[1] - 1
    later_log = later[:, head_dim:, :]
    total_log = prior[:, head_dim:, :] + later_log
    state = later[:, :head_dim, :] + jnp.exp(later_log) * prior[:, :head_dim, :]
    return jnp.concatenate([state, total_log], axis=1)


def exclusive_prefix(packed, axis):
    count = lax.axis_size(axis)
    before = jnp.zeros_like(packed)
    upto = packed
    stride = 1
    while stride < count:
        parts = [shifted(upto, axis, k * stride) for k in (3, 2, 1) if k * stride < count]
        older = parts[0]
        for part in parts[1:]:
            older = join_packed(older, part)
        before = join_packed(older, before)
        upto = join_packed(older, upto)
        stride *= 4
    return before


def rms_rows(values, gain):
    wide = values.astype(jnp.float32)
    return wide * lax.rsqrt(jnp.mean(wide * wide, axis=-1, keepdims=True) + EPS) * gain


def conv_four(rim, current, kernel):
    extended = jnp.concatenate([rim, current], axis=0).astype(jnp.float32)
    length = current.shape[0]
    result = kernel[0] * extended[0:length]
    for offset in range(1, 4):
        result = result + kernel[offset] * extended[offset : offset + length]
    return result


def local(
    tokens,
    norm1_gain,
    w_z,
    w_x,
    w_bc,
    w_dt,
    dt_bias,
    a_log,
    conv_x,
    conv_bc,
    d_skip,
    ssm_gain,
    w_out,
    norm2_gain,
    w_gate,
    w_up,
    w_down,
):
    gathered = lax.all_gather(tokens, "tp", axis=0, tiled=True)
    normed = rms_rows(gathered, norm1_gain).astype(jnp.bfloat16)
    bc_rows = jnp.dot(normed, w_bc, preferred_element_type=jnp.float32).astype(jnp.bfloat16)
    group_len = gathered.shape[0]
    head_count = w_dt.shape[1]
    channels = w_x.shape[1]
    gate_z = jnp.dot(normed, w_z, preferred_element_type=jnp.float32)
    inner_rows = jnp.dot(normed, w_x, preferred_element_type=jnp.float32).astype(jnp.bfloat16)
    dt_raw = jnp.dot(normed, w_dt, preferred_element_type=jnp.float32)
    rims = from_behind(jnp.concatenate([inner_rows[-3:], bc_rows[-3:]], axis=1), "ctx", 1)
    rim_inner, rim_bc = rims[:, :channels], rims[:, channels:]
    conv_inner = jax.nn.silu(conv_four(rim_inner, inner_rows, conv_x)).astype(jnp.bfloat16)
    conv_bcm = jax.nn.silu(conv_four(rim_bc, bc_rows, conv_bc)).astype(jnp.bfloat16)
    dt_step = jax.nn.softplus(dt_raw + dt_bias)
    log_decay = -dt_step * jnp.exp(a_log)
    block_count = group_len // BLOCK_LEN
    log_blocks = log_decay.reshape(block_count, BLOCK_LEN, head_count)
    step_blocks = dt_step.reshape(block_count, BLOCK_LEN, head_count)
    lower = jnp.tril(jnp.ones((BLOCK_LEN, BLOCK_LEN), jnp.float32))
    cum_decay = jnp.einsum("ts,bsh->bth", lower, log_blocks, precision=lax.Precision.HIGHEST)
    b_mat = conv_bcm[:, :STATE_DIM].reshape(block_count, BLOCK_LEN, STATE_DIM)
    c_mat = conv_bcm[:, STATE_DIM:].reshape(block_count, BLOCK_LEN, STATE_DIM)
    scores = jnp.einsum("btn,bsn->bts", c_mat, b_mat, preferred_element_type=jnp.float32)
    causal_mask = jnp.tril(jnp.ones((BLOCK_LEN, BLOCK_LEN), dtype=bool))[None, :, :, None]
    decay_diff = jnp.where(causal_mask, cum_decay[:, :, None, :] - cum_decay[:, None, :, :], 0.0)
    weights = jnp.where(causal_mask, jnp.exp(decay_diff), 0.0)
    inner_wide = conv_inner.astype(jnp.float32).reshape(
        block_count, BLOCK_LEN, head_count, HEAD_DIM
    )
    scaled = inner_wide * step_blocks[..., None]
    mixed_w = scores[..., None] * weights
    y_intra = jnp.einsum("btsh,bshp->bthp", mixed_w, scaled, precision=lax.Precision.HIGHEST)
    block_last = cum_decay[:, -1, :]
    tail_decay = jnp.exp(block_last[:, None, :] - cum_decay)
    b_wide = b_mat.astype(jnp.float32)
    c_wide = c_mat.astype(jnp.float32)
    block_states = jnp.einsum(
        "bsh,bshp,bsn->bhpn", tail_decay, scaled, b_wide, precision=lax.Precision.HIGHEST
    )
    block_decay = jnp.exp(block_last)
    zero_state = jnp.zeros((head_count, HEAD_DIM, STATE_DIM), jnp.float32)
    running = zero_state
    entering = []
    for block in range(block_count):
        entering.append(running)
        running = block_decay[block][:, None, None] * running + block_states[block]
    local_final, local_in = running, jnp.stack(entering)
    total_log = jnp.sum(block_last, axis=0)
    prior_decay = jnp.exp(jnp.cumsum(block_last, axis=0) - block_last)
    packed = jnp.concatenate(
        [local_final, jnp.broadcast_to(total_log[:, None, None], (head_count, 1, STATE_DIM))], axis=1
    )
    incoming = exclusive_prefix(packed, "ctx")[:, :HEAD_DIM, :]
    state_in = local_in + prior_decay[:, :, None, None] * incoming[None]
    y_inter = jnp.exp(cum_decay)[..., None] * jnp.einsum(
        "btn,bhpn->bthp", c_wide, state_in, precision=lax.Precision.HIGHEST
    )
    ssm_out = y_intra + y_inter + d_skip[None, None, :, None] * inner_wide
    gated = ssm_out.reshape(group_len, channels) * jax.nn.silu(gate_z)
    squares = jnp.sum(gated * gated, axis=-1)
    squares_hi = squares.astype(jnp.bfloat16)
    squares_lo = (squares - squares_hi.astype(jnp.float32)).astype(jnp.bfloat16)
    width = w_out.shape[1]
    pad_cols = 128
    extra = jnp.concatenate(
        [squares_hi[:, None], squares_lo[:, None]], axis=1
    ).astype(jnp.float32)
    extra = jnp.pad(extra, ((0, 0), (width, pad_cols - 2)))
    piece = (gated * ssm_gain).astype(jnp.bfloat16)
    w_out_wide = jnp.pad(w_out, ((0, 0), (0, pad_cols)))
    product = (jnp.dot(piece, w_out_wide, preferred_element_type=jnp.float32) + extra).astype(
        jnp.bfloat16
    )
    reduced = lax.psum_scatter(product, "tp", scatter_dimension=0, tiled=True)
    squares_own = reduced[:, width].astype(jnp.float32) + reduced[:, width + 1].astype(jnp.float32)
    scale = lax.rsqrt(squares_own / (HEADS * HEAD_DIM) + EPS)
    mixer_own = reduced[:, :width].astype(jnp.float32) * scale[:, None]
    resid = (tokens.astype(jnp.float32) + mixer_own).astype(jnp.bfloat16)
    normed_own = rms_rows(resid, norm2_gain).astype(jnp.bfloat16)
    mlp_in = lax.all_gather(normed_own, "tp", axis=0, tiled=True)
    mlp_gate = jnp.dot(mlp_in, w_gate, preferred_element_type=jnp.float32)
    mlp_up = jnp.dot(mlp_in, w_up, preferred_element_type=jnp.float32)
    hidden = (jax.nn.silu(mlp_gate) * mlp_up).astype(jnp.bfloat16)
    piece = hidden
    mlp_down = lax.psum_scatter(
        jnp.dot(piece, w_down, preferred_element_type=jnp.float32).astype(jnp.bfloat16),
        "tp",
        scatter_dimension=0,
        tiled=True,
    ).astype(jnp.float32)
    return (resid.astype(jnp.float32) + mlp_down).astype(jnp.bfloat16)


def solution(mesh):
    return jax.shard_map(
        local,
        mesh=mesh,
        in_specs=(
            P(("ctx", "tp"), None),
            P(),
            P(None, "tp"),
            P(None, "tp"),
            P(),
            P(None, "tp"),
            P("tp"),
            P("tp"),
            P(None, "tp"),
            P(),
            P("tp"),
            P("tp"),
            P("tp", None),
            P(),
            P(None, "tp"),
            P(None, "tp"),
            P("tp", None),
        ),
        out_specs=P(("ctx", "tp"), None),
        check_vma=False,
    )
```

```python
import jax
import jax.numpy as jnp
from jax import lax
from jax.sharding import PartitionSpec as P

HEADS = 80
HEAD_DIM = 64
STATE_DIM = 128
BLOCK_LEN = 256


EPS = 1e-05


def from_behind(value, axis, steps):
    count = lax.axis_size(axis)
    first, last = (max(0, -steps), min(count, count - steps))
    return lax.ppermute(value, axis, [(source, source + steps) for source in range(first, last)])


def shifted(value, axis, steps):
    count = lax.axis_size(axis)
    return lax.ppermute(value, axis, [(source, source + steps) for source in range(count - steps)])


def join_packed(prior, later):
    head_dim = later.shape[1] - 1
    later_log = later[:, head_dim:, :]
    total_log = prior[:, head_dim:, :] + later_log
    state = later[:, :head_dim, :] + jnp.exp(later_log) * prior[:, :head_dim, :]
    return jnp.concatenate([state, total_log], axis=1)


def exclusive_prefix(packed, axis):
    count = lax.axis_size(axis)
    before = jnp.zeros_like(packed)
    upto = packed
    stride = 1
    while stride < count:
        parts = [shifted(upto, axis, k * stride) for k in (3, 2, 1) if k * stride < count]
        older = parts[0]
        for part in parts[1:]:
            older = join_packed(older, part)
        before = join_packed(older, before)
        upto = join_packed(older, upto)
        stride *= 4
    return before


def rms_rows(values, gain):
    wide = values.astype(jnp.float32)
    return wide * lax.rsqrt(jnp.mean(wide * wide, axis=-1, keepdims=True) + EPS) * gain


def conv_four(rim, current, kernel):
    extended = jnp.concatenate([rim, current], axis=0).astype(jnp.float32)
    length = current.shape[0]
    result = kernel[0] * extended[0:length]
    for offset in range(1, 4):
        result = result + kernel[offset] * extended[offset : offset + length]
    return result


def local(
    tokens,
    norm1_gain,
    w_z,
    w_x,
    w_bc,
    w_dt,
    dt_bias,
    a_log,
    conv_x,
    conv_bc,
    d_skip,
    ssm_gain,
    w_out,
    norm2_gain,
    w_gate,
    w_up,
    w_down,
):
    gathered = lax.all_gather(tokens, "tp", axis=0, tiled=True)
    normed = rms_rows(gathered, norm1_gain).astype(jnp.bfloat16)
    bc_rows = jnp.dot(normed, w_bc, preferred_element_type=jnp.float32).astype(jnp.bfloat16)
    group_len = gathered.shape[0]
    head_count = w_dt.shape[1]
    channels = w_x.shape[1]
    gate_z = jnp.dot(normed, w_z, preferred_element_type=jnp.float32)
    inner_rows = jnp.dot(normed, w_x, preferred_element_type=jnp.float32).astype(jnp.bfloat16)
    dt_raw = jnp.dot(normed, w_dt, preferred_element_type=jnp.float32)
    rims = from_behind(jnp.concatenate([inner_rows[-3:], bc_rows[-3:]], axis=1), "ctx", 1)
    rim_inner, rim_bc = rims[:, :channels], rims[:, channels:]
    conv_inner = jax.nn.silu(conv_four(rim_inner, inner_rows, conv_x)).astype(jnp.bfloat16)
    conv_bcm = jax.nn.silu(conv_four(rim_bc, bc_rows, conv_bc)).astype(jnp.bfloat16)
    dt_step = jax.nn.softplus(dt_raw + dt_bias)
    log_decay = -dt_step * jnp.exp(a_log)
    block_count = group_len // BLOCK_LEN
    log_blocks = log_decay.reshape(block_count, BLOCK_LEN, head_count)
    step_blocks = dt_step.reshape(block_count, BLOCK_LEN, head_count)
    lower = jnp.tril(jnp.ones((BLOCK_LEN, BLOCK_LEN), jnp.float32))
    cum_decay = jnp.einsum("ts,bsh->bth", lower, log_blocks, precision=lax.Precision.HIGHEST)
    b_mat = conv_bcm[:, :STATE_DIM].reshape(block_count, BLOCK_LEN, STATE_DIM)
    c_mat = conv_bcm[:, STATE_DIM:].reshape(block_count, BLOCK_LEN, STATE_DIM)
    scores = jnp.einsum("btn,bsn->bts", c_mat, b_mat, preferred_element_type=jnp.float32)
    causal_mask = jnp.tril(jnp.ones((BLOCK_LEN, BLOCK_LEN), dtype=bool))[None, :, :, None]
    decay_diff = jnp.where(causal_mask, cum_decay[:, :, None, :] - cum_decay[:, None, :, :], 0.0)
    weights = jnp.where(causal_mask, jnp.exp(decay_diff), 0.0)
    inner_wide = conv_inner.astype(jnp.float32).reshape(
        block_count, BLOCK_LEN, head_count, HEAD_DIM
    )
    scaled = inner_wide * step_blocks[..., None]
    mixed_w = scores[..., None] * weights
    y_intra = jnp.einsum("btsh,bshp->bthp", mixed_w, scaled, precision=lax.Precision.HIGHEST)
    block_last = cum_decay[:, -1, :]
    tail_decay = jnp.exp(block_last[:, None, :] - cum_decay)
    b_wide = b_mat.astype(jnp.float32)
    c_wide = c_mat.astype(jnp.float32)
    block_states = jnp.einsum(
        "bsh,bshp,bsn->bhpn", tail_decay, scaled, b_wide, precision=lax.Precision.HIGHEST
    )
    block_decay = jnp.exp(block_last)
    zero_state = jnp.zeros((head_count, HEAD_DIM, STATE_DIM), jnp.float32)
    running = zero_state
    entering = []
    for block in range(block_count):
        entering.append(running)
        running = block_decay[block][:, None, None] * running + block_states[block]
    local_final, local_in = running, jnp.stack(entering)
    total_log = jnp.sum(block_last, axis=0)
    prior_decay = jnp.exp(jnp.cumsum(block_last, axis=0) - block_last)
    packed = jnp.concatenate(
        [local_final, jnp.broadcast_to(total_log[:, None, None], (head_count, 1, STATE_DIM))], axis=1
    )
    incoming = exclusive_prefix(packed, "ctx")[:, :HEAD_DIM, :]
    state_in = local_in + prior_decay[:, :, None, None] * incoming[None]
    y_inter = jnp.exp(cum_decay)[..., None] * jnp.einsum(
        "btn,bhpn->bthp", c_wide, state_in, precision=lax.Precision.HIGHEST
    )
    ssm_out = y_intra + y_inter + d_skip[None, None, :, None] * inner_wide
    gated = ssm_out.reshape(group_len, channels) * jax.nn.silu(gate_z)
    squares = jnp.sum(gated * gated, axis=-1)
    squares_hi = squares.astype(jnp.bfloat16)
    squares_lo = (squares - squares_hi.astype(jnp.float32)).astype(jnp.bfloat16)
    width = w_out.shape[1]
    pad_cols = 128
    extra = jnp.concatenate(
        [squares_hi[:, None], squares_lo[:, None]], axis=1
    ).astype(jnp.float32)
    extra = jnp.pad(extra, ((0, 0), (width, pad_cols - 2)))
    piece = (gated * ssm_gain).astype(jnp.bfloat16)
    w_out_wide = jnp.pad(w_out, ((0, 0), (0, pad_cols)))
    product = (jnp.dot(piece, w_out_wide, preferred_element_type=jnp.float32) + extra).astype(
        jnp.bfloat16
    )
    reduced = lax.psum_scatter(product, "tp", scatter_dimension=0, tiled=True)
    squares_own = reduced[:, width].astype(jnp.float32) + reduced[:, width + 1].astype(jnp.float32)
    scale = lax.rsqrt(squares_own / (HEADS * HEAD_DIM) + EPS)
    mixer_own = reduced[:, :width].astype(jnp.float32) * scale[:, None]
    resid = (tokens.astype(jnp.float32) + mixer_own).astype(jnp.bfloat16)
    normed_own = rms_rows(resid, norm2_gain).astype(jnp.bfloat16)
    halves = 2
    rows = normed_own.shape[0] // halves
    outs = []
    for half in range(halves):
        own = slice(half * rows, (half + 1) * rows)
        mlp_in = lax.all_gather(normed_own[own], "tp", axis=0, tiled=True)
        mlp_gate = jnp.dot(mlp_in, w_gate, preferred_element_type=jnp.float32)
        mlp_up = jnp.dot(mlp_in, w_up, preferred_element_type=jnp.float32)
        hidden = (jax.nn.silu(mlp_gate) * mlp_up).astype(jnp.bfloat16)
        mlp_down = lax.psum_scatter(
            jnp.dot(hidden, w_down, preferred_element_type=jnp.float32).astype(jnp.bfloat16),
            "tp",
            scatter_dimension=0,
            tiled=True,
        ).astype(jnp.float32)
        outs.append((resid[own].astype(jnp.float32) + mlp_down).astype(jnp.bfloat16))
    return jnp.concatenate(outs, axis=0)


def solution(mesh):
    return jax.shard_map(
        local,
        mesh=mesh,
        in_specs=(
            P(("ctx", "tp"), None),
            P(),
            P(None, "tp"),
            P(None, "tp"),
            P(),
            P(None, "tp"),
            P("tp"),
            P("tp"),
            P(None, "tp"),
            P(),
            P("tp"),
            P("tp"),
            P("tp", None),
            P(),
            P(None, "tp"),
            P(None, "tp"),
            P("tp", None),
        ),
        out_specs=P(("ctx", "tp"), None),
        check_vma=False,
    )
```

```python
import jax
import jax.numpy as jnp
from jax import lax
from jax.sharding import PartitionSpec as P

HEADS = 80
HEAD_DIM = 64
STATE_DIM = 128
BLOCK_LEN = 256


EPS = 1e-05


def from_behind(value, axis, steps):
    count = lax.axis_size(axis)
    first, last = (max(0, -steps), min(count, count - steps))
    return lax.ppermute(value, axis, [(source, source + steps) for source in range(first, last)])


def shifted(value, axis, steps):
    count = lax.axis_size(axis)
    return lax.ppermute(value, axis, [(source, source + steps) for source in range(count - steps)])


def join_packed(prior, later):
    head_dim = later.shape[1] - 1
    later_log = later[:, head_dim:, :]
    total_log = prior[:, head_dim:, :] + later_log
    state = later[:, :head_dim, :] + jnp.exp(later_log) * prior[:, :head_dim, :]
    return jnp.concatenate([state, total_log], axis=1)


def exclusive_prefix(packed, axis):
    count = lax.axis_size(axis)
    before = jnp.zeros_like(packed)
    upto = packed
    stride = 1
    while stride < count:
        parts = [shifted(upto, axis, k * stride) for k in (3, 2, 1) if k * stride < count]
        older = parts[0]
        for part in parts[1:]:
            older = join_packed(older, part)
        before = join_packed(older, before)
        upto = join_packed(older, upto)
        stride *= 4
    return before


def rms_rows(values, gain):
    wide = values.astype(jnp.float32)
    return wide * lax.rsqrt(jnp.mean(wide * wide, axis=-1, keepdims=True) + EPS) * gain


def conv_four(rim, current, kernel):
    extended = jnp.concatenate([rim, current], axis=0).astype(jnp.float32)
    length = current.shape[0]
    result = kernel[0] * extended[0:length]
    for offset in range(1, 4):
        result = result + kernel[offset] * extended[offset : offset + length]
    return result


def local(
    tokens,
    norm1_gain,
    w_z,
    w_x,
    w_bc,
    w_dt,
    dt_bias,
    a_log,
    conv_x,
    conv_bc,
    d_skip,
    ssm_gain,
    w_out,
    norm2_gain,
    w_gate,
    w_up,
    w_down,
):
    gathered = lax.all_gather(tokens, "tp", axis=0, tiled=True)
    normed = rms_rows(gathered, norm1_gain).astype(jnp.bfloat16)
    bc_rows = jnp.dot(normed, w_bc, preferred_element_type=jnp.float32).astype(jnp.bfloat16)
    group_len = gathered.shape[0]
    head_count = w_dt.shape[1]
    channels = w_x.shape[1]
    gate_z = jnp.dot(normed, w_z, preferred_element_type=jnp.float32)
    inner_rows = jnp.dot(normed, w_x, preferred_element_type=jnp.float32).astype(jnp.bfloat16)
    dt_raw = jnp.dot(normed, w_dt, preferred_element_type=jnp.float32)
    rims = from_behind(jnp.concatenate([inner_rows[-3:], bc_rows[-3:]], axis=1), "ctx", 1)
    rim_inner, rim_bc = rims[:, :channels], rims[:, channels:]
    conv_inner = jax.nn.silu(conv_four(rim_inner, inner_rows, conv_x)).astype(jnp.bfloat16)
    conv_bcm = jax.nn.silu(conv_four(rim_bc, bc_rows, conv_bc)).astype(jnp.bfloat16)
    dt_step = jax.nn.softplus(dt_raw + dt_bias)
    log_decay = -dt_step * jnp.exp(a_log)
    block_count = group_len // BLOCK_LEN
    log_blocks = log_decay.reshape(block_count, BLOCK_LEN, head_count)
    step_blocks = dt_step.reshape(block_count, BLOCK_LEN, head_count)
    lower = jnp.tril(jnp.ones((BLOCK_LEN, BLOCK_LEN), jnp.float32))
    cum_decay = jnp.einsum("ts,bsh->bth", lower, log_blocks, precision=lax.Precision.HIGH)
    b_mat = conv_bcm[:, :STATE_DIM].reshape(block_count, BLOCK_LEN, STATE_DIM)
    c_mat = conv_bcm[:, STATE_DIM:].reshape(block_count, BLOCK_LEN, STATE_DIM)
    scores = jnp.einsum("btn,bsn->bts", c_mat, b_mat, preferred_element_type=jnp.float32)
    causal_mask = jnp.tril(jnp.ones((BLOCK_LEN, BLOCK_LEN), dtype=bool))[None, :, :, None]
    decay_diff = jnp.where(causal_mask, cum_decay[:, :, None, :] - cum_decay[:, None, :, :], 0.0)
    weights = jnp.where(causal_mask, jnp.exp(decay_diff), 0.0)
    inner_wide = conv_inner.astype(jnp.float32).reshape(
        block_count, BLOCK_LEN, head_count, HEAD_DIM
    )
    scaled = inner_wide * step_blocks[..., None]
    mixed_w = scores[..., None] * weights
    y_intra = jnp.einsum("btsh,bshp->bthp", mixed_w, scaled, precision=lax.Precision.HIGH)
    block_last = cum_decay[:, -1, :]
    tail_decay = jnp.exp(block_last[:, None, :] - cum_decay)
    b_wide = b_mat.astype(jnp.float32)
    c_wide = c_mat.astype(jnp.float32)
    block_states = jnp.einsum(
        "bsh,bshp,bsn->bhpn", tail_decay, scaled, b_wide, precision=lax.Precision.HIGH
    )
    block_decay = jnp.exp(block_last)
    zero_state = jnp.zeros((head_count, HEAD_DIM, STATE_DIM), jnp.float32)
    running = zero_state
    entering = []
    for block in range(block_count):
        entering.append(running)
        running = block_decay[block][:, None, None] * running + block_states[block]
    local_final, local_in = running, jnp.stack(entering)
    total_log = jnp.sum(block_last, axis=0)
    prior_decay = jnp.exp(jnp.cumsum(block_last, axis=0) - block_last)
    packed = jnp.concatenate(
        [local_final, jnp.broadcast_to(total_log[:, None, None], (head_count, 1, STATE_DIM))], axis=1
    )
    incoming = exclusive_prefix(packed, "ctx")[:, :HEAD_DIM, :]
    state_in = local_in + prior_decay[:, :, None, None] * incoming[None]
    y_inter = jnp.exp(cum_decay)[..., None] * jnp.einsum(
        "btn,bhpn->bthp", c_wide, state_in, precision=lax.Precision.HIGH
    )
    ssm_out = y_intra + y_inter + d_skip[None, None, :, None] * inner_wide
    gated = ssm_out.reshape(group_len, channels) * jax.nn.silu(gate_z)
    squares = jnp.sum(gated * gated, axis=-1)
    squares_hi = squares.astype(jnp.bfloat16)
    squares_lo = (squares - squares_hi.astype(jnp.float32)).astype(jnp.bfloat16)
    width = w_out.shape[1]
    pad_cols = 128
    extra = jnp.concatenate(
        [squares_hi[:, None], squares_lo[:, None]], axis=1
    ).astype(jnp.float32)
    extra = jnp.pad(extra, ((0, 0), (width, pad_cols - 2)))
    piece = (gated * ssm_gain).astype(jnp.bfloat16)
    w_out_wide = jnp.pad(w_out, ((0, 0), (0, pad_cols)))
    product = (jnp.dot(piece, w_out_wide, preferred_element_type=jnp.float32) + extra).astype(
        jnp.bfloat16
    )
    reduced = lax.psum_scatter(product, "tp", scatter_dimension=0, tiled=True)
    squares_own = reduced[:, width].astype(jnp.float32) + reduced[:, width + 1].astype(jnp.float32)
    scale = lax.rsqrt(squares_own / (HEADS * HEAD_DIM) + EPS)
    mixer_own = reduced[:, :width].astype(jnp.float32) * scale[:, None]
    resid = (tokens.astype(jnp.float32) + mixer_own).astype(jnp.bfloat16)
    normed_own = rms_rows(resid, norm2_gain).astype(jnp.bfloat16)
    mlp_in = lax.all_gather(normed_own, "tp", axis=0, tiled=True)
    mlp_gate = jnp.dot(mlp_in, w_gate, preferred_element_type=jnp.float32)
    mlp_up = jnp.dot(mlp_in, w_up, preferred_element_type=jnp.float32)
    hidden = (jax.nn.silu(mlp_gate) * mlp_up).astype(jnp.bfloat16)
    piece = hidden
    mlp_down = lax.psum_scatter(
        jnp.dot(piece, w_down, preferred_element_type=jnp.float32).astype(jnp.bfloat16),
        "tp",
        scatter_dimension=0,
        tiled=True,
    ).astype(jnp.float32)
    return (resid.astype(jnp.float32) + mlp_down).astype(jnp.bfloat16)


def solution(mesh):
    return jax.shard_map(
        local,
        mesh=mesh,
        in_specs=(
            P(("ctx", "tp"), None),
            P(),
            P(None, "tp"),
            P(None, "tp"),
            P(),
            P(None, "tp"),
            P("tp"),
            P("tp"),
            P(None, "tp"),
            P(),
            P("tp"),
            P("tp"),
            P("tp", None),
            P(),
            P(None, "tp"),
            P(None, "tp"),
            P("tp", None),
        ),
        out_specs=P(("ctx", "tp"), None),
        check_vma=False,
    )
```

```python
import jax
import jax.numpy as jnp
from jax import lax
from jax.sharding import PartitionSpec as P

HEADS = 80
HEAD_DIM = 64
STATE_DIM = 128
BLOCK_LEN = 256


EPS = 1e-05


def from_behind(value, axis, steps):
    count = lax.axis_size(axis)
    first, last = (max(0, -steps), min(count, count - steps))
    return lax.ppermute(value, axis, [(source, source + steps) for source in range(first, last)])


def shifted(value, axis, steps):
    count = lax.axis_size(axis)
    return lax.ppermute(value, axis, [(source, source + steps) for source in range(count - steps)])


def join_packed(prior, later):
    head_dim = later.shape[1] - 1
    later_log = later[:, head_dim:, :]
    total_log = prior[:, head_dim:, :] + later_log
    state = later[:, :head_dim, :] + jnp.exp(later_log) * prior[:, :head_dim, :]
    return jnp.concatenate([state, total_log], axis=1)


def exclusive_prefix(packed, axis):
    count = lax.axis_size(axis)
    upto = shifted(packed, axis, 1)
    stride = 1
    while stride < count:
        upto = join_packed(shifted(upto, axis, stride), upto)
        stride *= 2
    return upto


def rms_rows(values, gain):
    wide = values.astype(jnp.float32)
    return wide * lax.rsqrt(jnp.mean(wide * wide, axis=-1, keepdims=True) + EPS) * gain


def conv_four(rim, current, kernel):
    extended = jnp.concatenate([rim, current], axis=0).astype(jnp.float32)
    length = current.shape[0]
    result = kernel[0] * extended[0:length]
    for offset in range(1, 4):
        result = result + kernel[offset] * extended[offset : offset + length]
    return result


def local(
    tokens,
    norm1_gain,
    w_z,
    w_x,
    w_bc,
    w_dt,
    dt_bias,
    a_log,
    conv_x,
    conv_bc,
    d_skip,
    ssm_gain,
    w_out,
    norm2_gain,
    w_gate,
    w_up,
    w_down,
):
    gathered = lax.all_gather(tokens, "tp", axis=0, tiled=True)
    normed = rms_rows(gathered, norm1_gain).astype(jnp.bfloat16)
    bc_rows = jnp.dot(normed, w_bc, preferred_element_type=jnp.float32).astype(jnp.bfloat16)
    group_len = gathered.shape[0]
    head_count = w_dt.shape[1]
    channels = w_x.shape[1]
    gate_z = jnp.dot(normed, w_z, preferred_element_type=jnp.float32)
    inner_rows = jnp.dot(normed, w_x, preferred_element_type=jnp.float32).astype(jnp.bfloat16)
    dt_raw = jnp.dot(normed, w_dt, preferred_element_type=jnp.float32)
    rims = from_behind(jnp.concatenate([inner_rows[-3:], bc_rows[-3:]], axis=1), "ctx", 1)
    rim_inner, rim_bc = rims[:, :channels], rims[:, channels:]
    conv_inner = jax.nn.silu(conv_four(rim_inner, inner_rows, conv_x)).astype(jnp.bfloat16)
    conv_bcm = jax.nn.silu(conv_four(rim_bc, bc_rows, conv_bc)).astype(jnp.bfloat16)
    dt_step = jax.nn.softplus(dt_raw + dt_bias)
    log_decay = -dt_step * jnp.exp(a_log)
    block_count = group_len // BLOCK_LEN
    log_blocks = log_decay.reshape(block_count, BLOCK_LEN, head_count)
    step_blocks = dt_step.reshape(block_count, BLOCK_LEN, head_count)
    lower = jnp.tril(jnp.ones((BLOCK_LEN, BLOCK_LEN), jnp.float32))
    cum_decay = jnp.einsum("ts,bsh->bth", lower, log_blocks, precision=lax.Precision.HIGH)
    b_mat = conv_bcm[:, :STATE_DIM].reshape(block_count, BLOCK_LEN, STATE_DIM)
    c_mat = conv_bcm[:, STATE_DIM:].reshape(block_count, BLOCK_LEN, STATE_DIM)
    scores = jnp.einsum("btn,bsn->bts", c_mat, b_mat, preferred_element_type=jnp.float32)
    causal_mask = jnp.tril(jnp.ones((BLOCK_LEN, BLOCK_LEN), dtype=bool))[None, :, :, None]
    decay_diff = jnp.where(causal_mask, cum_decay[:, :, None, :] - cum_decay[:, None, :, :], 0.0)
    weights = jnp.where(causal_mask, jnp.exp(decay_diff), 0.0)
    inner_wide = conv_inner.astype(jnp.float32).reshape(
        block_count, BLOCK_LEN, head_count, HEAD_DIM
    )
    scaled = inner_wide * step_blocks[..., None]
    mixed_w = scores[..., None] * weights
    y_intra = jnp.einsum("btsh,bshp->bthp", mixed_w, scaled, precision=lax.Precision.HIGH)
    block_last = cum_decay[:, -1, :]
    tail_decay = jnp.exp(block_last[:, None, :] - cum_decay)
    b_wide = b_mat.astype(jnp.float32)
    c_wide = c_mat.astype(jnp.float32)
    block_states = jnp.einsum(
        "bsh,bshp,bsn->bhpn", tail_decay, scaled, b_wide, precision=lax.Precision.HIGH
    )
    block_decay = jnp.exp(block_last)
    zero_state = jnp.zeros((head_count, HEAD_DIM, STATE_DIM), jnp.float32)
    running = zero_state
    entering = []
    for block in range(block_count):
        entering.append(running)
        running = block_decay[block][:, None, None] * running + block_states[block]
    local_final, local_in = running, jnp.stack(entering)
    total_log = jnp.sum(block_last, axis=0)
    prior_decay = jnp.exp(jnp.cumsum(block_last, axis=0) - block_last)
    packed = jnp.concatenate(
        [local_final, jnp.broadcast_to(total_log[:, None, None], (head_count, 1, STATE_DIM))], axis=1
    )
    incoming = exclusive_prefix(packed, "ctx")[:, :HEAD_DIM, :]
    state_in = local_in + prior_decay[:, :, None, None] * incoming[None]
    y_inter = jnp.exp(cum_decay)[..., None] * jnp.einsum(
        "btn,bhpn->bthp", c_wide, state_in, precision=lax.Precision.HIGH
    )
    ssm_out = y_intra + y_inter + d_skip[None, None, :, None] * inner_wide
    gated = ssm_out.reshape(group_len, channels) * jax.nn.silu(gate_z)
    squares = jnp.sum(gated * gated, axis=-1)
    squares_hi = squares.astype(jnp.bfloat16)
    squares_lo = (squares - squares_hi.astype(jnp.float32)).astype(jnp.bfloat16)
    width = w_out.shape[1]
    pad_cols = 128
    extra = jnp.concatenate(
        [squares_hi[:, None], squares_lo[:, None]], axis=1
    ).astype(jnp.float32)
    extra = jnp.pad(extra, ((0, 0), (width, pad_cols - 2)))
    piece = (gated * ssm_gain).astype(jnp.bfloat16)
    w_out_wide = jnp.pad(w_out, ((0, 0), (0, pad_cols)))
    product = (jnp.dot(piece, w_out_wide, preferred_element_type=jnp.float32) + extra).astype(
        jnp.bfloat16
    )
    reduced = lax.psum_scatter(product, "tp", scatter_dimension=0, tiled=True)
    squares_own = reduced[:, width].astype(jnp.float32) + reduced[:, width + 1].astype(jnp.float32)
    scale = lax.rsqrt(squares_own / (HEADS * HEAD_DIM) + EPS)
    mixer_own = reduced[:, :width].astype(jnp.float32) * scale[:, None]
    resid = (tokens.astype(jnp.float32) + mixer_own).astype(jnp.bfloat16)
    normed_own = rms_rows(resid, norm2_gain).astype(jnp.bfloat16)
    mlp_in = lax.all_gather(normed_own, "tp", axis=0, tiled=True)
    mlp_gate = jnp.dot(mlp_in, w_gate, preferred_element_type=jnp.float32)
    mlp_up = jnp.dot(mlp_in, w_up, preferred_element_type=jnp.float32)
    hidden = (jax.nn.silu(mlp_gate) * mlp_up).astype(jnp.bfloat16)
    piece = hidden
    mlp_down = lax.psum_scatter(
        jnp.dot(piece, w_down, preferred_element_type=jnp.float32).astype(jnp.bfloat16),
        "tp",
        scatter_dimension=0,
        tiled=True,
    ).astype(jnp.float32)
    return (resid.astype(jnp.float32) + mlp_down).astype(jnp.bfloat16)


def solution(mesh):
    return jax.shard_map(
        local,
        mesh=mesh,
        in_specs=(
            P(("ctx", "tp"), None),
            P(),
            P(None, "tp"),
            P(None, "tp"),
            P(),
            P(None, "tp"),
            P("tp"),
            P("tp"),
            P(None, "tp"),
            P(),
            P("tp"),
            P("tp"),
            P("tp", None),
            P(),
            P(None, "tp"),
            P(None, "tp"),
            P("tp", None),
        ),
        out_specs=P(("ctx", "tp"), None),
        check_vma=False,
    )
```

```python
import jax
import jax.numpy as jnp
from jax import lax
from jax.sharding import PartitionSpec as P

HEADS = 80
HEAD_DIM = 64
STATE_DIM = 128
BLOCK_LEN = 256


EPS = 1e-05


def from_behind(value, axis, steps):
    count = lax.axis_size(axis)
    first, last = (max(0, -steps), min(count, count - steps))
    return lax.ppermute(value, axis, [(source, source + steps) for source in range(first, last)])


def shifted(value, axis, steps):
    count = lax.axis_size(axis)
    return lax.ppermute(value, axis, [(source, source + steps) for source in range(count - steps)])


def join_packed(prior, later):
    head_dim = later.shape[1] - 1
    later_log = later[:, head_dim:, :]
    total_log = prior[:, head_dim:, :] + later_log
    state = later[:, :head_dim, :] + jnp.exp(later_log) * prior[:, :head_dim, :]
    return jnp.concatenate([state, total_log], axis=1)


def exclusive_prefix(packed, axis):
    count = lax.axis_size(axis)
    before = jnp.zeros_like(packed)
    upto = packed
    stride = 1
    while stride < count:
        parts = [shifted(upto, axis, k * stride) for k in (3, 2, 1) if k * stride < count]
        older = parts[0]
        for part in parts[1:]:
            older = join_packed(older, part)
        before = join_packed(older, before)
        upto = join_packed(older, upto)
        stride *= 4
    return before


def rms_rows(values, gain):
    wide = values.astype(jnp.float32)
    return wide * lax.rsqrt(jnp.mean(wide * wide, axis=-1, keepdims=True) + EPS) * gain


def conv_four(rim, current, kernel):
    extended = jnp.concatenate([rim, current], axis=0).astype(jnp.float32)
    length = current.shape[0]
    result = kernel[0] * extended[0:length]
    for offset in range(1, 4):
        result = result + kernel[offset] * extended[offset : offset + length]
    return result


def local(
    tokens,
    norm1_gain,
    w_z,
    w_x,
    w_bc,
    w_dt,
    dt_bias,
    a_log,
    conv_x,
    conv_bc,
    d_skip,
    ssm_gain,
    w_out,
    norm2_gain,
    w_gate,
    w_up,
    w_down,
):
    gathered = lax.all_gather(tokens, "tp", axis=0, tiled=True)
    normed = rms_rows(gathered, norm1_gain).astype(jnp.bfloat16)
    bc_rows = jnp.dot(normed, w_bc, preferred_element_type=jnp.float32).astype(jnp.bfloat16)
    group_len = gathered.shape[0]
    head_count = w_dt.shape[1]
    channels = w_x.shape[1]
    gate_z = jnp.dot(normed, w_z, preferred_element_type=jnp.float32)
    inner_rows = jnp.dot(normed, w_x, preferred_element_type=jnp.float32).astype(jnp.bfloat16)
    dt_raw = jnp.dot(normed, w_dt, preferred_element_type=jnp.float32)
    rims = from_behind(jnp.concatenate([inner_rows[-3:], bc_rows[-3:]], axis=1), "ctx", 1)
    rim_inner, rim_bc = rims[:, :channels], rims[:, channels:]
    conv_inner = jax.nn.silu(conv_four(rim_inner, inner_rows, conv_x)).astype(jnp.bfloat16)
    conv_bcm = jax.nn.silu(conv_four(rim_bc, bc_rows, conv_bc)).astype(jnp.bfloat16)
    dt_step = jax.nn.softplus(dt_raw + dt_bias)
    log_decay = -dt_step * jnp.exp(a_log)
    block_count = group_len // BLOCK_LEN
    log_blocks = log_decay.reshape(block_count, BLOCK_LEN, head_count)
    step_blocks = dt_step.reshape(block_count, BLOCK_LEN, head_count)
    lower = jnp.tril(jnp.ones((BLOCK_LEN, BLOCK_LEN), jnp.float32))
    cum_decay = jnp.einsum("ts,bsh->bth", lower, log_blocks, precision=lax.Precision.HIGH)
    b_mat = conv_bcm[:, :STATE_DIM].reshape(block_count, BLOCK_LEN, STATE_DIM)
    c_mat = conv_bcm[:, STATE_DIM:].reshape(block_count, BLOCK_LEN, STATE_DIM)
    scores = jnp.einsum("btn,bsn->bts", c_mat, b_mat, preferred_element_type=jnp.float32)
    causal_mask = jnp.tril(jnp.ones((BLOCK_LEN, BLOCK_LEN), dtype=bool))[None, :, :, None]
    decay_diff = jnp.where(causal_mask, cum_decay[:, :, None, :] - cum_decay[:, None, :, :], 0.0)
    weights = jnp.where(causal_mask, jnp.exp(decay_diff), 0.0)
    inner_wide = conv_inner.astype(jnp.float32).reshape(
        block_count, BLOCK_LEN, head_count, HEAD_DIM
    )
    scaled = inner_wide * step_blocks[..., None]
    mixed_w = scores[..., None] * weights
    y_intra = jnp.einsum("btsh,bshp->bthp", mixed_w, scaled, precision=lax.Precision.HIGH)
    block_last = cum_decay[:, -1, :]
    tail_decay = jnp.exp(block_last[:, None, :] - cum_decay)
    b_wide = b_mat.astype(jnp.float32)
    c_wide = c_mat.astype(jnp.float32)
    block_states = jnp.einsum(
        "bsh,bshp,bsn->bhpn", tail_decay, scaled, b_wide, precision=lax.Precision.HIGH
    )
    block_decay = jnp.exp(block_last)
    zero_state = jnp.zeros((head_count, HEAD_DIM, STATE_DIM), jnp.float32)
    running = zero_state
    entering = []
    for block in range(block_count):
        entering.append(running)
        running = block_decay[block][:, None, None] * running + block_states[block]
    local_final, local_in = running, jnp.stack(entering)
    total_log = jnp.sum(block_last, axis=0)
    prior_decay = jnp.exp(jnp.cumsum(block_last, axis=0) - block_last)
    packed = jnp.concatenate(
        [local_final, jnp.broadcast_to(total_log[:, None, None], (head_count, 1, STATE_DIM))], axis=1
    )
    incoming = exclusive_prefix(packed, "ctx")[:, :HEAD_DIM, :]
    state_in = local_in + prior_decay[:, :, None, None] * incoming[None]
    y_inter = jnp.exp(cum_decay)[..., None] * jnp.einsum(
        "btn,bhpn->bthp", c_wide, state_in, precision=lax.Precision.HIGH
    )
    ssm_out = y_intra + y_inter + d_skip[None, None, :, None] * inner_wide
    gated = ssm_out.reshape(group_len, channels) * jax.nn.silu(gate_z)
    squares = jnp.sum(gated * gated, axis=-1)
    squares_hi = squares.astype(jnp.bfloat16)
    squares_lo = (squares - squares_hi.astype(jnp.float32)).astype(jnp.bfloat16)
    width = w_out.shape[1]
    pad_cols = 128
    extra = jnp.concatenate(
        [squares_hi[:, None], squares_lo[:, None], jnp.zeros((group_len, pad_cols - 2), jnp.bfloat16)],
        axis=1,
    )
    piece = jnp.concatenate([(gated * ssm_gain).astype(jnp.bfloat16), extra], axis=1)
    lane = lax.broadcasted_iota(jnp.int32, (pad_cols, pad_cols), 1)
    sub = lax.broadcasted_iota(jnp.int32, (pad_cols, pad_cols), 0)
    pick = ((lane == sub) & (sub < 2)).astype(jnp.bfloat16)
    w_out_wide = jnp.concatenate(
        [
            jnp.pad(w_out, ((0, 0), (0, pad_cols))),
            jnp.concatenate([jnp.zeros((pad_cols, width), jnp.bfloat16), pick], axis=1),
        ],
        axis=0,
    )
    product = jnp.dot(piece, w_out_wide, preferred_element_type=jnp.float32).astype(jnp.bfloat16)
    reduced = lax.psum_scatter(product, "tp", scatter_dimension=0, tiled=True)
    squares_own = reduced[:, width].astype(jnp.float32) + reduced[:, width + 1].astype(jnp.float32)
    scale = lax.rsqrt(squares_own / (HEADS * HEAD_DIM) + EPS)
    mixer_own = reduced[:, :width].astype(jnp.float32) * scale[:, None]
    own_rows = tokens.shape[0]
    own_tokens = lax.dynamic_slice_in_dim(gathered, lax.axis_index("tp") * own_rows, own_rows, 0)
    resid = (own_tokens.astype(jnp.float32) + mixer_own).astype(jnp.bfloat16)
    normed_own = rms_rows(resid, norm2_gain).astype(jnp.bfloat16)
    mlp_in = lax.all_gather(normed_own, "tp", axis=0, tiled=True)
    mlp_gate = jnp.dot(mlp_in, w_gate, preferred_element_type=jnp.float32)
    mlp_up = jnp.dot(mlp_in, w_up, preferred_element_type=jnp.float32)
    hidden = (jax.nn.silu(mlp_gate) * mlp_up).astype(jnp.bfloat16)
    piece = hidden
    mlp_down = lax.psum_scatter(
        jnp.dot(piece, w_down, preferred_element_type=jnp.float32).astype(jnp.bfloat16),
        "tp",
        scatter_dimension=0,
        tiled=True,
    ).astype(jnp.float32)
    return (resid.astype(jnp.float32) + mlp_down).astype(jnp.bfloat16)


def solution(mesh):
    return jax.shard_map(
        local,
        mesh=mesh,
        in_specs=(
            P(("ctx", "tp"), None),
            P(),
            P(None, "tp"),
            P(None, "tp"),
            P(),
            P(None, "tp"),
            P("tp"),
            P("tp"),
            P(None, "tp"),
            P(),
            P("tp"),
            P("tp"),
            P("tp", None),
            P(),
            P(None, "tp"),
            P(None, "tp"),
            P("tp", None),
        ),
        out_specs=P(("ctx", "tp"), None),
        check_vma=False,
    )
```

```python
import jax
import jax.numpy as jnp
from jax import lax
from jax.sharding import PartitionSpec as P

HEADS = 80
HEAD_DIM = 64
STATE_DIM = 128
BLOCK_LEN = 256


EPS = 1e-05


def from_behind(value, axis, steps):
    count = lax.axis_size(axis)
    first, last = (max(0, -steps), min(count, count - steps))
    return lax.ppermute(value, axis, [(source, source + steps) for source in range(first, last)])


def shifted(value, axis, steps):
    count = lax.axis_size(axis)
    return lax.ppermute(value, axis, [(source, source + steps) for source in range(count - steps)])


def join_packed(prior, later):
    head_dim = later.shape[1] - 1
    later_log = later[:, head_dim:, :]
    total_log = prior[:, head_dim:, :] + later_log
    state = later[:, :head_dim, :] + jnp.exp(later_log) * prior[:, :head_dim, :]
    return jnp.concatenate([state, total_log], axis=1)


def exclusive_prefix(packed, axis):
    count = lax.axis_size(axis)
    before = jnp.zeros_like(packed)
    upto = packed
    stride = 1
    while stride < count:
        parts = [shifted(upto, axis, k * stride) for k in (3, 2, 1) if k * stride < count]
        older = parts[0]
        for part in parts[1:]:
            older = join_packed(older, part)
        before = join_packed(older, before)
        upto = join_packed(older, upto)
        stride *= 4
    return before


def rms_rows(values, gain):
    wide = values.astype(jnp.float32)
    return wide * lax.rsqrt(jnp.mean(wide * wide, axis=-1, keepdims=True) + EPS) * gain


def conv_four(rim, current, kernel):
    extended = jnp.concatenate([rim, current], axis=0).astype(jnp.float32)
    length = current.shape[0]
    result = kernel[0] * extended[0:length]
    for offset in range(1, 4):
        result = result + kernel[offset] * extended[offset : offset + length]
    return result


def local(
    tokens,
    norm1_gain,
    w_z,
    w_x,
    w_bc,
    w_dt,
    dt_bias,
    a_log,
    conv_x,
    conv_bc,
    d_skip,
    ssm_gain,
    w_out,
    norm2_gain,
    w_gate,
    w_up,
    w_down,
):
    wide = tokens.astype(jnp.float32)
    own_scale = lax.rsqrt(jnp.mean(wide * wide, axis=-1) + EPS)
    scale_top = lax.reduce_precision(own_scale, exponent_bits=8, mantissa_bits=7)
    scale_hi = scale_top.astype(jnp.bfloat16)
    scale_lo = (own_scale - scale_top).astype(jnp.bfloat16)
    width_in = tokens.shape[1]
    payload = jnp.concatenate(
        [tokens, scale_hi[:, None], scale_lo[:, None], jnp.zeros((tokens.shape[0], 126), jnp.bfloat16)],
        axis=1,
    )
    gathered_all = lax.all_gather(payload, "tp", axis=0, tiled=True)
    gathered = gathered_all[:, :width_in]
    row_scale = gathered_all[:, width_in].astype(jnp.float32) + gathered_all[:, width_in + 1].astype(
        jnp.float32
    )
    normed = (gathered.astype(jnp.float32) * row_scale[:, None] * norm1_gain).astype(jnp.bfloat16)
    bc_rows = jnp.dot(normed, w_bc, preferred_element_type=jnp.float32).astype(jnp.bfloat16)
    group_len = gathered.shape[0]
    head_count = w_dt.shape[1]
    channels = w_x.shape[1]
    gate_z = jnp.dot(normed, w_z, preferred_element_type=jnp.float32)
    inner_rows = jnp.dot(normed, w_x, preferred_element_type=jnp.float32).astype(jnp.bfloat16)
    dt_raw = jnp.dot(normed, w_dt, preferred_element_type=jnp.float32)
    rims = from_behind(jnp.concatenate([inner_rows[-3:], bc_rows[-3:]], axis=1), "ctx", 1)
    rim_inner, rim_bc = rims[:, :channels], rims[:, channels:]
    conv_inner = jax.nn.silu(conv_four(rim_inner, inner_rows, conv_x)).astype(jnp.bfloat16)
    conv_bcm = jax.nn.silu(conv_four(rim_bc, bc_rows, conv_bc)).astype(jnp.bfloat16)
    dt_step = jax.nn.softplus(dt_raw + dt_bias)
    log_decay = -dt_step * jnp.exp(a_log)
    block_count = group_len // BLOCK_LEN
    log_blocks = log_decay.reshape(block_count, BLOCK_LEN, head_count)
    step_blocks = dt_step.reshape(block_count, BLOCK_LEN, head_count)
    lower = jnp.tril(jnp.ones((BLOCK_LEN, BLOCK_LEN), jnp.float32))
    cum_decay = jnp.einsum("ts,bsh->bth", lower, log_blocks, precision=lax.Precision.HIGH)
    b_mat = conv_bcm[:, :STATE_DIM].reshape(block_count, BLOCK_LEN, STATE_DIM)
    c_mat = conv_bcm[:, STATE_DIM:].reshape(block_count, BLOCK_LEN, STATE_DIM)
    scores = jnp.einsum("btn,bsn->bts", c_mat, b_mat, preferred_element_type=jnp.float32)
    causal_mask = jnp.tril(jnp.ones((BLOCK_LEN, BLOCK_LEN), dtype=bool))[None, :, :, None]
    decay_diff = jnp.where(causal_mask, cum_decay[:, :, None, :] - cum_decay[:, None, :, :], 0.0)
    weights = jnp.where(causal_mask, jnp.exp(decay_diff), 0.0)
    inner_wide = conv_inner.astype(jnp.float32).reshape(
        block_count, BLOCK_LEN, head_count, HEAD_DIM
    )
    scaled = inner_wide * step_blocks[..., None]
    mixed_w = scores[..., None] * weights
    y_intra = jnp.einsum("btsh,bshp->bthp", mixed_w, scaled, precision=lax.Precision.HIGH)
    block_last = cum_decay[:, -1, :]
    tail_decay = jnp.exp(block_last[:, None, :] - cum_decay)
    b_wide = b_mat.astype(jnp.float32)
    c_wide = c_mat.astype(jnp.float32)
    block_states = jnp.einsum(
        "bsh,bshp,bsn->bhpn", tail_decay, scaled, b_wide, precision=lax.Precision.HIGH
    )
    block_decay = jnp.exp(block_last)
    zero_state = jnp.zeros((head_count, HEAD_DIM, STATE_DIM), jnp.float32)
    running = zero_state
    entering = []
    for block in range(block_count):
        entering.append(running)
        running = block_decay[block][:, None, None] * running + block_states[block]
    local_final, local_in = running, jnp.stack(entering)
    total_log = jnp.sum(block_last, axis=0)
    prior_decay = jnp.exp(jnp.cumsum(block_last, axis=0) - block_last)
    packed = jnp.concatenate(
        [local_final, jnp.broadcast_to(total_log[:, None, None], (head_count, 1, STATE_DIM))], axis=1
    )
    incoming = exclusive_prefix(packed, "ctx")[:, :HEAD_DIM, :]
    state_in = local_in + prior_decay[:, :, None, None] * incoming[None]
    y_inter = jnp.exp(cum_decay)[..., None] * jnp.einsum(
        "btn,bhpn->bthp", c_wide, state_in, precision=lax.Precision.HIGH
    )
    ssm_out = y_intra + y_inter + d_skip[None, None, :, None] * inner_wide
    gated = ssm_out.reshape(group_len, channels) * jax.nn.silu(gate_z)
    squares = jnp.sum(gated * gated, axis=-1)
    squares_hi = squares.astype(jnp.bfloat16)
    squares_lo = (squares - squares_hi.astype(jnp.float32)).astype(jnp.bfloat16)
    width = w_out.shape[1]
    pad_cols = 128
    extra = jnp.concatenate(
        [squares_hi[:, None], squares_lo[:, None], jnp.zeros((group_len, pad_cols - 2), jnp.bfloat16)],
        axis=1,
    )
    piece = jnp.concatenate([(gated * ssm_gain).astype(jnp.bfloat16), extra], axis=1)
    lane = lax.broadcasted_iota(jnp.int32, (pad_cols, pad_cols), 1)
    sub = lax.broadcasted_iota(jnp.int32, (pad_cols, pad_cols), 0)
    pick = ((lane == sub) & (sub < 2)).astype(jnp.bfloat16)
    w_out_wide = jnp.concatenate(
        [
            jnp.pad(w_out, ((0, 0), (0, pad_cols))),
            jnp.concatenate([jnp.zeros((pad_cols, width), jnp.bfloat16), pick], axis=1),
        ],
        axis=0,
    )
    product = jnp.dot(piece, w_out_wide, preferred_element_type=jnp.float32).astype(jnp.bfloat16)
    reduced = lax.psum_scatter(product, "tp", scatter_dimension=0, tiled=True)
    squares_own = reduced[:, width].astype(jnp.float32) + reduced[:, width + 1].astype(jnp.float32)
    scale = lax.rsqrt(squares_own / (HEADS * HEAD_DIM) + EPS)
    mixer_own = reduced[:, :width].astype(jnp.float32) * scale[:, None]
    own_rows = tokens.shape[0]
    own_tokens = lax.dynamic_slice_in_dim(gathered_all, lax.axis_index("tp") * own_rows, own_rows, 0)
    own_tokens = own_tokens[:, :width_in]
    resid = (own_tokens.astype(jnp.float32) + mixer_own).astype(jnp.bfloat16)
    normed_own = rms_rows(resid, norm2_gain).astype(jnp.bfloat16)
    mlp_in = lax.all_gather(normed_own, "tp", axis=0, tiled=True)
    mlp_gate = jnp.dot(mlp_in, w_gate, preferred_element_type=jnp.float32)
    mlp_up = jnp.dot(mlp_in, w_up, preferred_element_type=jnp.float32)
    hidden = (jax.nn.silu(mlp_gate) * mlp_up).astype(jnp.bfloat16)
    piece = hidden
    mlp_down = lax.psum_scatter(
        jnp.dot(piece, w_down, preferred_element_type=jnp.float32).astype(jnp.bfloat16),
        "tp",
        scatter_dimension=0,
        tiled=True,
    ).astype(jnp.float32)
    return (resid.astype(jnp.float32) + mlp_down).astype(jnp.bfloat16)


def solution(mesh):
    return jax.shard_map(
        local,
        mesh=mesh,
        in_specs=(
            P(("ctx", "tp"), None),
            P(),
            P(None, "tp"),
            P(None, "tp"),
            P(),
            P(None, "tp"),
            P("tp"),
            P("tp"),
            P(None, "tp"),
            P(),
            P("tp"),
            P("tp"),
            P("tp", None),
            P(),
            P(None, "tp"),
            P(None, "tp"),
            P("tp", None),
        ),
        out_specs=P(("ctx", "tp"), None),
        check_vma=False,
    )
```
